768 devices in a mesh: tm: 12 (over z), dp: 64 (over y, x, core).
Axes of the slice: x: 4, y: 8, z: 12, core: 2. Of those that a mesh axis runs over, the one named last changes fastest.
Arguments:
- clip_video: bfloat16 [64, 24, 4, 16, 192], P('dp', 'tm'), may hold values from -6 to 6
- clip_ids: int32 [64, 24], P('dp'), may hold values from 0 to 3, never falling along the last dimension, each value on 1 to 12 neighbouring positions
- norm_gain: float32 [192], replicated, may hold values from 0.25 to 1.75
- conv_weight: bfloat16 [5184, 384], replicated, may hold values from -0.078125 to 0.078125
- out_cotangent: bfloat16 [64, 24, 4, 16, 384], P('dp', 'tm'), may hold values from -16 to 16
Outputs:
- conv_out: bfloat16 [64, 24, 4, 16, 384], P('dp', 'tm')
- grad_video: bfloat16 [64, 24, 4, 16, 192], P('dp', 'tm')
- grad_weight: float32 [5184, 384], P('tm', 'dp')
The draws below stay inside these ranges and needn't reach their ends.
Inputs may be any that keep to these rules, and one draw needn't show every extreme that they name: `clip_ids`: within each group clip numbers never fall along the frames; each clip lasts 1 to 12 frames and one lasts exactly 12.
All inputs are finite; a program needn't handle non-finite values.
Results may differ from the reference program's by a relative error of at most 0.0049.
Values may be sent and summed in bfloat16 or wider, within the bound.
No kernel may reach another device: no remote copies, remote signals or barrier semaphores. Data moves between devices by JAX's collectives and lax.ppermute only.
A program may use at most 32 MiB of HBM per device.

```python
import math
import jax
import jax.numpy as jnp
import numpy as np
from jax import lax

C_IN = 192
C_OUT = 384
H = 4
W = 16
KROWS = 5184
FRAMES = 24
GROUPS = 64


def with_spikes(result, own_key, source, target, shards_of, factor):
    owner, partner = [(jnp.arange(result.shape[position]) // (result.shape[position] // shards_of)).reshape([-1 if axis == position else 1 for axis in range(result.ndim)]) for position in (source, target)]
    chosen = jax.random.permutation(own_key, shards_of)[partner]
    strong = (owner == chosen) | (owner == (partner + shards_of // 2) % shards_of)
    return jnp.where(strong, factor * result, result)


def block_scale(key, extent, pieces, low, largest):
    def one(position, parts):
        heights = jax.random.uniform(jax.random.fold_in(jax.random.fold_in(key, 6), position), (parts,), jnp.float32, low / len(pieces), largest / len(pieces))
        return jnp.repeat(jnp.exp(heights), extent[position] // parts).reshape((-1,) + (1,) * (len(extent) - position - 1))

    loudness = one(*pieces[0])
    for cut in pieces[1:]:
        loudness = loudness * one(*cut)
    return loudness


def split_up(number_of, total, reach, slope):
    portions = [(1 << 20) // math.isqrt(standing ** slope) + 1 for standing in range(2, number_of + 1)]
    spare, counts = total - reach - (number_of - 1), [1] * (number_of - 1)
    while spare > 0:
        movable = [i for i in range(number_of - 1) if counts[i] < reach]
        whole, left = sum([portions[i] for i in movable]), spare
        for i in movable:
            more = min(reach - counts[i], max(1, left * portions[i] // whole), spare)
            counts[i] = counts[i] + more
            spare = spare - more
    return np.array([reach] + counts)


def uneven(key, amount, total, limit, skew):
    if amount == 2:
        one = jax.random.randint(key, (), max(1, total - limit), min(limit, total - 1) + 1)
        return jnp.stack([one, total - one])
    lengths = jnp.asarray(split_up(amount, total, limit, skew), jnp.int32)
    pairs = (amount - 1) // 2
    giver, sink = lengths[1:1 + 2 * pairs:2], lengths[2:2 + 2 * pairs:2]
    slack = jnp.minimum(giver - 1, limit - sink)
    shifted = jax.random.randint(jax.random.fold_in(key, 1), (pairs,), 0, 1 << 20) % (slack + 1)
    lengths = lengths.at[1:1 + 2 * pairs:2].set(giver - shifted).at[2:2 + 2 * pairs:2].set(sink + shifted)
    return lengths[jax.random.permutation(jax.random.fold_in(key, 2), amount)]


def centred(key, extent, scale, most, shards=(), kind=jnp.bfloat16):
    factor_of = block_scale(key, extent, shards, -0.22, 0.18) if shards else 1.0
    values = jax.random.normal(key, extent, jnp.float32) * scale * factor_of
    return jnp.minimum(jnp.maximum(values, -most), most).astype(kind)


def heavy_noise(key, dims, deviation, reach, cuts, heavy, held_as=jnp.bfloat16):
    array = deviation * jax.random.normal(key, dims, jnp.float32)
    if cuts:
        array = array * block_scale(key, dims, cuts, -0.22, 0.18)
    return jnp.clip(with_spikes(array, jax.random.fold_in(key, 3), *heavy), -reach, reach).astype(held_as)


def setup_inputs(seed: int = 0) -> dict:
    arg_keys = jax.random.split(jax.random.key(seed), 6)
    return {
        "clip_video": centred(arg_keys[0], (GROUPS, FRAMES, H, W, C_IN), 1.0, 6.0, ((0, 64), (1, 12))),
        "clip_ids": jax.vmap(lambda own: jnp.searchsorted(jnp.cumsum(uneven(own, 4, FRAMES, FRAMES // 2, 1)), jnp.arange(FRAMES), side="right"))(jax.random.split(arg_keys[1], GROUPS)).reshape((GROUPS, FRAMES)).astype(jnp.int32),
        "norm_gain": jnp.clip(1.0 + 0.15 * jax.random.normal(arg_keys[2], (C_IN,), jnp.float32), 0.25, 1.75),
        "conv_weight": centred(arg_keys[3], (KROWS, C_OUT), KROWS ** -0.5, 0.078125),
        "out_cotangent": heavy_noise(arg_keys[4], (GROUPS, FRAMES, H, W, C_OUT), 1.0, 16.0, ((0, 64), (1, 12)), (0, 4, 64, 4.0)),
    }


def activate(video, norm_gain):
    values = video.astype(jnp.float32)
    mean_square = lax.optimization_barrier(jnp.mean(values * values, axis=-1, keepdims=True))
    normed = values * lax.rsqrt(mean_square + 1e-06) * norm_gain
    return jax.nn.silu(normed)

def make_mask(clips, first_frame, count):
    padded_ids = jnp.concatenate([jnp.full((2,), -1, jnp.int32), clips.astype(jnp.int32)])
    window = lax.dynamic_slice_in_dim(padded_ids, first_frame, count + 2)
    offsets = jnp.arange(count)[:, None] + jnp.arange(3)[None, :]
    current = window[jnp.arange(count) + 2][:, None]
    return (window[offsets] == current).astype(jnp.float32)

def extract(extended, tap_mask):
    frames = tap_mask.shape[0]
    height, width = (extended.shape[1], extended.shape[2])
    padded = jnp.pad(extended, ((0, 0), (1, 1), (1, 1), (0, 0)))
    taps = []
    for tap_t in range(3):
        weight_t = tap_mask[:, tap_t][:, None, None, None].astype(extended.dtype)
        for tap_h in range(3):
            for tap_w in range(3):
                taps.append(padded[tap_t:tap_t + frames, tap_h:tap_h + height, tap_w:tap_w + width] * weight_t)
    stacked = jnp.stack(taps, axis=3)
    return stacked.reshape(frames * height * width, -1)

def reference(clip_video, clip_ids, norm_gain, conv_weight, out_cotangent):
    frames, height, width, channels = clip_video.shape[1:]
    outputs = conv_weight.shape[1]

    def one_group(weight_sum, items):
        video, cotangent, clips = items
        activated = activate(video, norm_gain).astype(jnp.bfloat16)
        extended = jnp.concatenate([jnp.zeros((2, height, width, channels), jnp.bfloat16), activated])
        tap_mask = make_mask(clips, 0, frames)
        patches = extract(extended, tap_mask)
        conv_rows = jnp.dot(patches, conv_weight, preferred_element_type=jnp.float32).astype(jnp.bfloat16)
        cotangent_rows = cotangent.reshape(-1, outputs)
        weight_sum = weight_sum + jnp.dot(patches.T, cotangent_rows, preferred_element_type=jnp.float32)
        patch_grad = jnp.dot(cotangent_rows, conv_weight.T, preferred_element_type=jnp.float32)
        unused, pull_patch = jax.vjp(lambda field: extract(field, tap_mask), extended.astype(jnp.float32))
        extended_grad = pull_patch(patch_grad)[0]
        unused, pull_norm = jax.vjp(lambda field: activate(field, norm_gain), video.astype(jnp.float32))
        video_grad = pull_norm(extended_grad[2:])[0].astype(jnp.bfloat16)
        return (weight_sum, (conv_rows.reshape(frames, height, width, outputs), video_grad))
    start_sum = jnp.zeros(conv_weight.shape, jnp.float32)
    weight_sum, (conv_out, grad_video) = lax.scan(one_group, start_sum, (clip_video, out_cotangent, clip_ids))
    scale = 1.0 / math.sqrt(clip_video.shape[0] * frames * height * width)
    return (conv_out, grad_video, weight_sum * scale)
```

```python
import math

import jax
import jax.numpy as jnp
from jax import lax
from jax.sharding import PartitionSpec as P


def from_behind(block, axis, distance):
    devices = range(lax.axis_size(axis))
    route = [(i - distance, i) for i in devices if i - distance in devices]
    return lax.ppermute(block, axis, route)


def activate(video, norm_gain):
    values = video.astype(jnp.float32)
    mean_square = jnp.mean(values * values, axis=-1, keepdims=True)
    normed = values * lax.rsqrt(mean_square + 1e-06) * norm_gain
    return jax.nn.silu(normed)


def make_mask(clips, first_frame, count):
    padded_ids = jnp.concatenate([jnp.full((2,), -1, jnp.int32), clips])
    window = lax.dynamic_slice_in_dim(padded_ids, first_frame, count + 2)
    offsets = jnp.arange(count)[:, None] + jnp.arange(3)[None, :]
    current = window[jnp.arange(count) + 2][:, None]
    return (window[offsets] == current).astype(jnp.float32)


def extract(extended, tap_mask):
    frames = tap_mask.shape[0]
    height, width = (extended.shape[1], extended.shape[2])
    padded = jnp.pad(extended, ((0, 0), (1, 1), (1, 1), (0, 0)))
    taps = []
    for tap_t in range(3):
        weight_t = tap_mask[:, tap_t][:, None, None, None].astype(extended.dtype)
        for tap_h in range(3):
            for tap_w in range(3):
                taps.append(
                    padded[tap_t : tap_t + frames, tap_h : tap_h + height, tap_w : tap_w + width]
                    * weight_t
                )
    stacked = jnp.stack(taps, axis=3)
    return stacked.reshape(frames * height * width, -1)


def shards(clip_video, clip_ids, norm_gain, conv_weight, out_cotangent):
    video = clip_video[0]
    frames, height, width, channels = video.shape
    outputs = conv_weight.shape[1]
    activated = activate(video, norm_gain).astype(jnp.bfloat16)
    previous = from_behind(activated, "tm", 1)
    extended = jnp.concatenate([previous, activated])
    first_frame = lax.axis_index("tm") * frames
    tap_mask = make_mask(clip_ids[0], first_frame, frames)
    patches = extract(extended, tap_mask)
    conv_rows = jnp.dot(patches, conv_weight, preferred_element_type=jnp.float32).astype(
        jnp.bfloat16
    )
    cotangent_rows = out_cotangent[0].reshape(-1, outputs)
    patch_grad = jnp.dot(cotangent_rows, conv_weight.T, preferred_element_type=jnp.float32)
    unused, pull_patch = jax.vjp(
        lambda field: extract(field, tap_mask), extended.astype(jnp.float32)
    )
    extended_grad = pull_patch(patch_grad)[0]
    returned = from_behind(extended_grad[:2], "tm", -1)
    own_grad = extended_grad[2:] + returned
    unused, pull_norm = jax.vjp(lambda field: activate(field, norm_gain), video.astype(jnp.float32))
    video_grad = pull_norm(own_grad)[0].astype(jnp.bfloat16)
    chain_len = lax.axis_size("tm")
    scale = 1.0 / math.sqrt(lax.axis_size("dp") * chain_len * frames * height * width)
    kernel_rows = patches.shape[1]
    slab_rows = kernel_rows // chain_len
    slab_start = lax.axis_index("tm") * slab_rows
    tap_lo = slab_start // channels
    slab_offset = slab_start - tap_lo * channels
    group_video = lax.all_gather(activated, "tm", axis=0, tiled=True)
    group_cot = lax.all_gather(out_cotangent[0], "tm", axis=0, tiled=True)
    group_frames = group_video.shape[0]
    group_mask = make_mask(clip_ids[0], 0, group_frames).astype(jnp.bfloat16)
    group_pad = jnp.pad(group_video, ((2, 0), (1, 1), (1, 1), (0, 0)))
    tap_count = -(-(slab_rows + channels - 1) // channels)
    columns = []
    for step in range(tap_count):
        tap = jnp.minimum(tap_lo + step, 26)
        tap_t, tap_h, tap_w = (tap // 9, tap // 3 % 3, tap % 3)
        window = lax.dynamic_slice(
            group_pad, (tap_t, tap_h, tap_w, 0), (group_frames, height, width, channels)
        )
        weight_t = lax.dynamic_index_in_dim(group_mask, tap_t, 1, keepdims=False)
        columns.append((window * weight_t[:, None, None, None]).reshape(-1, channels))
    slab_patches = lax.dynamic_slice_in_dim(jnp.concatenate(columns, axis=1), slab_offset, slab_rows, 1)
    slab_t = lax.dot_general(
        group_cot.reshape(-1, outputs),
        slab_patches,
        (((0,), (0,)), ((), ())),
        preferred_element_type=jnp.float32,
    )
    reduced_t = lax.psum_scatter(slab_t, "dp", scatter_dimension=0, tiled=True)
    grad_weight = reduced_t.T * scale
    conv_out = conv_rows.reshape(1, frames, height, width, outputs)
    return (conv_out, video_grad[None], grad_weight)


def solution(mesh):
    in_specs = (
        P("dp", "tm", None, None, None),
        P("dp", None),
        P(),
        P(),
        P("dp", "tm", None, None, None),
    )
    out_specs = (P("dp", "tm", None, None, None), P("dp", "tm", None, None, None), P("tm", "dp"))
    return jax.shard_map(shards, mesh=mesh, in_specs=in_specs, out_specs=out_specs, check_vma=False)
```

```python
import math

import jax
import jax.numpy as jnp
from jax import lax
from jax.sharding import PartitionSpec as P


def from_behind(block, axis, distance):
    devices = range(lax.axis_size(axis))
    route = [(i - distance, i) for i in devices if i - distance in devices]
    return lax.ppermute(block, axis, route)


def activate(video, norm_gain):
    values = video.astype(jnp.float32)
    mean_square = jnp.mean(values * values, axis=-1, keepdims=True)
    normed = values * lax.rsqrt(mean_square + 1e-06) * norm_gain
    return jax.nn.silu(normed)


def make_mask(clips, first_frame, count):
    padded_ids = jnp.concatenate([jnp.full((2,), -1, jnp.int32), clips])
    window = lax.dynamic_slice_in_dim(padded_ids, first_frame, count + 2)
    offsets = jnp.arange(count)[:, None] + jnp.arange(3)[None, :]
    current = window[jnp.arange(count) + 2][:, None]
    return (window[offsets] == current).astype(jnp.float32)


def extract(extended, tap_mask):
    frames = tap_mask.shape[0]
    height, width = (extended.shape[1], extended.shape[2])
    padded = jnp.pad(extended, ((0, 0), (1, 1), (1, 1), (0, 0)))
    taps = []
    for tap_t in range(3):
        weight_t = tap_mask[:, tap_t][:, None, None, None].astype(extended.dtype)
        for tap_h in range(3):
            for tap_w in range(3):
                taps.append(
                    padded[tap_t : tap_t + frames, tap_h : tap_h + height, tap_w : tap_w + width]
                    * weight_t
                )
    stacked = jnp.stack(taps, axis=3)
    return stacked.reshape(frames * height * width, -1)


def shards(clip_video, clip_ids, norm_gain, conv_weight, out_cotangent):
    video = clip_video[0]
    frames, height, width, channels = video.shape
    outputs = conv_weight.shape[1]
    activated = activate(video, norm_gain).astype(jnp.bfloat16)
    previous = from_behind(activated, "tm", 1)
    extended = jnp.concatenate([previous, activated])
    first_frame = lax.axis_index("tm") * frames
    tap_mask = make_mask(clip_ids[0], first_frame, frames)
    patches = extract(extended, tap_mask)
    conv_rows = jnp.dot(patches, conv_weight, preferred_element_type=jnp.float32).astype(
        jnp.bfloat16
    )
    cotangent_rows = out_cotangent[0].reshape(-1, outputs)
    patch_grad = jnp.dot(cotangent_rows, conv_weight.T, preferred_element_type=jnp.float32)
    unused, pull_patch = jax.vjp(
        lambda field: extract(field, tap_mask), extended.astype(jnp.float32)
    )
    extended_grad = pull_patch(patch_grad)[0]
    returned = from_behind(extended_grad[:2], "tm", -1)
    own_grad = extended_grad[2:] + returned
    unused, pull_norm = jax.vjp(lambda field: activate(field, norm_gain), video.astype(jnp.float32))
    video_grad = pull_norm(own_grad)[0].astype(jnp.bfloat16)
    chain_len = lax.axis_size("tm")
    scale = 1.0 / math.sqrt(lax.axis_size("dp") * chain_len * frames * height * width)
    kernel_rows = patches.shape[1]
    slab_rows = kernel_rows // chain_len
    slab_start = lax.axis_index("tm") * slab_rows
    tap_lo = slab_start // channels
    slab_offset = slab_start - tap_lo * channels
    group_both = lax.all_gather(
        jnp.concatenate([activated, out_cotangent[0]], axis=-1), "tm", axis=0, tiled=True
    )
    group_video = group_both[..., :channels]
    group_cot = group_both[..., channels:]
    group_frames = group_video.shape[0]
    group_mask = make_mask(clip_ids[0], 0, group_frames).astype(jnp.bfloat16)
    group_pad = jnp.pad(group_video, ((2, 0), (1, 1), (1, 1), (0, 0)))
    tap_count = -(-(slab_rows + channels - 1) // channels)
    columns = []
    for step in range(tap_count):
        tap = jnp.minimum(tap_lo + step, 26)
        tap_t, tap_h, tap_w = (tap // 9, tap // 3 % 3, tap % 3)
        window = lax.dynamic_slice(
            group_pad, (tap_t, tap_h, tap_w, 0), (group_frames, height, width, channels)
        )
        weight_t = lax.dynamic_index_in_dim(group_mask, tap_t, 1, keepdims=False)
        columns.append((window * weight_t[:, None, None, None]).reshape(-1, channels))
    slab_patches = lax.dynamic_slice_in_dim(jnp.concatenate(columns, axis=1), slab_offset, slab_rows, 1)
    slab_t = lax.dot_general(
        group_cot.reshape(-1, outputs),
        slab_patches,
        (((0,), (0,)), ((), ())),
        preferred_element_type=jnp.float32,
    )
    groups = lax.axis_size("dp")
    pieces = slab_t.reshape(groups, outputs // groups, slab_rows)
    reduced_t = lax.all_to_all(pieces, "dp", 0, 0, tiled=False).sum(axis=0)
    grad_weight = reduced_t.T * scale
    conv_out = conv_rows.reshape(1, frames, height, width, outputs)
    return (conv_out, video_grad[None], grad_weight)


def solution(mesh):
    in_specs = (
        P("dp", "tm", None, None, None),
        P("dp", None),
        P(),
        P(),
        P("dp", "tm", None, None, None),
    )
    out_specs = (P("dp", "tm", None, None, None), P("dp", "tm", None, None, None), P("tm", "dp"))
    return jax.shard_map(shards, mesh=mesh, in_specs=in_specs, out_specs=out_specs, check_vma=False)
```

```python
import math

import jax
import jax.numpy as jnp
from jax import lax
from jax.sharding import PartitionSpec as P


def from_behind(block, axis, distance):
    devices = range(lax.axis_size(axis))
    route = [(i - distance, i) for i in devices if i - distance in devices]
    return lax.ppermute(block, axis, route)


def activate(video, norm_gain):
    values = video.astype(jnp.float32)
    mean_square = jnp.mean(values * values, axis=-1, keepdims=True)
    normed = values * lax.rsqrt(mean_square + 1e-06) * norm_gain
    return jax.nn.silu(normed)


def make_mask(clips, first_frame, count):
    padded_ids = jnp.concatenate([jnp.full((2,), -1, jnp.int32), clips])
    window = lax.dynamic_slice_in_dim(padded_ids, first_frame, count + 2)
    offsets = jnp.arange(count)[:, None] + jnp.arange(3)[None, :]
    current = window[jnp.arange(count) + 2][:, None]
    return (window[offsets] == current).astype(jnp.float32)


def extract(extended, tap_mask):
    frames = tap_mask.shape[0]
    height, width = (extended.shape[1], extended.shape[2])
    padded = jnp.pad(extended, ((0, 0), (1, 1), (1, 1), (0, 0)))
    taps = []
    for tap_t in range(3):
        weight_t = tap_mask[:, tap_t][:, None, None, None].astype(extended.dtype)
        for tap_h in range(3):
            for tap_w in range(3):
                taps.append(
                    padded[tap_t : tap_t + frames, tap_h : tap_h + height, tap_w : tap_w + width]
                    * weight_t
                )
    stacked = jnp.stack(taps, axis=3)
    return stacked.reshape(frames * height * width, -1)


def shards(clip_video, clip_ids, norm_gain, conv_weight, out_cotangent):
    video = clip_video[0]
    frames, height, width, channels = video.shape
    outputs = conv_weight.shape[1]
    activated = activate(video, norm_gain).astype(jnp.bfloat16)
    previous = from_behind(activated, "tm", 1)
    extended = jnp.concatenate([previous, activated])
    first_frame = lax.axis_index("tm") * frames
    tap_mask = make_mask(clip_ids[0], first_frame, frames)
    patches = extract(extended, tap_mask)
    conv_rows = jnp.dot(patches, conv_weight, preferred_element_type=jnp.float32).astype(
        jnp.bfloat16
    )
    cotangent_rows = out_cotangent[0].reshape(-1, outputs)
    patch_grad = jnp.dot(cotangent_rows, conv_weight.T, preferred_element_type=jnp.float32)
    unused, pull_patch = jax.vjp(
        lambda field: extract(field, tap_mask), extended.astype(jnp.float32)
    )
    extended_grad = pull_patch(patch_grad)[0]
    returned = from_behind(extended_grad[:2], "tm", -1)
    own_grad = extended_grad[2:] + returned
    unused, pull_norm = jax.vjp(lambda field: activate(field, norm_gain), video.astype(jnp.float32))
    video_grad = pull_norm(own_grad)[0].astype(jnp.bfloat16)
    chain_len = lax.axis_size("tm")
    scale = 1.0 / math.sqrt(lax.axis_size("dp") * chain_len * frames * height * width)
    kernel_rows = patches.shape[1]
    slab_rows = kernel_rows // chain_len
    slab_start = lax.axis_index("tm") * slab_rows
    tap_lo = slab_start // channels
    slab_offset = slab_start - tap_lo * channels
    group_both = lax.all_gather(
        jnp.concatenate([video, out_cotangent[0]], axis=-1), "tm", axis=0, tiled=True
    )
    group_video = activate(group_both[..., :channels], norm_gain).astype(jnp.bfloat16)
    group_cot = group_both[..., channels:]
    group_frames = group_video.shape[0]
    group_mask = make_mask(clip_ids[0], 0, group_frames).astype(jnp.bfloat16)
    group_pad = jnp.pad(group_video, ((2, 0), (1, 1), (1, 1), (0, 0)))
    tap_count = -(-(slab_rows + channels - 1) // channels)
    columns = []
    for step in range(tap_count):
        tap = jnp.minimum(tap_lo + step, 26)
        tap_t, tap_h, tap_w = (tap // 9, tap // 3 % 3, tap % 3)
        window = lax.dynamic_slice(
            group_pad, (tap_t, tap_h, tap_w, 0), (group_frames, height, width, channels)
        )
        weight_t = lax.dynamic_index_in_dim(group_mask, tap_t, 1, keepdims=False)
        columns.append((window * weight_t[:, None, None, None]).reshape(-1, channels))
    slab_patches = lax.dynamic_slice_in_dim(jnp.concatenate(columns, axis=1), slab_offset, slab_rows, 1)
    slab_t = lax.dot_general(
        group_cot.reshape(-1, outputs),
        slab_patches,
        (((0,), (0,)), ((), ())),
        preferred_element_type=jnp.float32,
    )
    groups = lax.axis_size("dp")
    pieces = slab_t.reshape(groups, outputs // groups, slab_rows)
    reduced_t = lax.all_to_all(pieces, "dp", 0, 0, tiled=False).sum(axis=0)
    grad_weight = reduced_t.T * scale
    conv_out = conv_rows.reshape(1, frames, height, width, outputs)
    return (conv_out, video_grad[None], grad_weight)


def solution(mesh):
    in_specs = (
        P("dp", "tm", None, None, None),
        P("dp", None),
        P(),
        P(),
        P("dp", "tm", None, None, None),
    )
    out_specs = (P("dp", "tm", None, None, None), P("dp", "tm", None, None, None), P("tm", "dp"))
    return jax.shard_map(shards, mesh=mesh, in_specs=in_specs, out_specs=out_specs, check_vma=False)
```

```python
import math

import jax
import jax.numpy as jnp
from jax import lax
from jax.sharding import PartitionSpec as P


def from_behind(block, axis, distance):
    devices = range(lax.axis_size(axis))
    route = [(i - distance, i) for i in devices if i - distance in devices]
    return lax.ppermute(block, axis, route)


def ring_route(axis, step):
    size = lax.axis_size(axis)
    return [(i, (i + step) % size) for i in range(size)]


def ring_gather(block, axis, first_behind):
    size = lax.axis_size(axis)
    from_ahead = []
    from_behind_list = [first_behind]
    for unused in range(size // 2 - 1):
        from_behind_list.append(lax.ppermute(from_behind_list[-1], axis, ring_route(axis, 1)))
    moving = block
    for unused in range(size - 1 - size // 2):
        moving = lax.ppermute(moving, axis, ring_route(axis, -1))
        from_ahead.append(moving)
    relative = [block] + from_ahead + from_behind_list[::-1]
    stacked = jnp.stack(relative, axis=0)
    ordered = jnp.roll(stacked, lax.axis_index(axis), axis=0)
    return ordered.reshape((-1,) + block.shape[1:])


def activate(video, norm_gain):
    values = video.astype(jnp.float32)
    mean_square = jnp.mean(values * values, axis=-1, keepdims=True)
    normed = values * lax.rsqrt(mean_square + 1e-06) * norm_gain
    return jax.nn.silu(normed)


def make_mask(clips, first_frame, count):
    padded_ids = jnp.concatenate([jnp.full((2,), -1, jnp.int32), clips])
    window = lax.dynamic_slice_in_dim(padded_ids, first_frame, count + 2)
    offsets = jnp.arange(count)[:, None] + jnp.arange(3)[None, :]
    current = window[jnp.arange(count) + 2][:, None]
    return (window[offsets] == current).astype(jnp.float32)


def extract(extended, tap_mask):
    frames = tap_mask.shape[0]
    height, width = (extended.shape[1], extended.shape[2])
    padded = jnp.pad(extended, ((0, 0), (1, 1), (1, 1), (0, 0)))
    taps = []
    for tap_t in range(3):
        weight_t = tap_mask[:, tap_t][:, None, None, None].astype(extended.dtype)
        for tap_h in range(3):
            for tap_w in range(3):
                taps.append(
                    padded[tap_t : tap_t + frames, tap_h : tap_h + height, tap_w : tap_w + width]
                    * weight_t
                )
    stacked = jnp.stack(taps, axis=3)
    return stacked.reshape(frames * height * width, -1)


def shards(clip_video, clip_ids, norm_gain, conv_weight, out_cotangent):
    video = clip_video[0]
    frames, height, width, channels = video.shape
    outputs = conv_weight.shape[1]
    activated = activate(video, norm_gain).astype(jnp.bfloat16)
    both = jnp.concatenate([video, out_cotangent[0]], axis=-1)
    first_behind = lax.ppermute(both, "tm", ring_route("tm", 1))
    previous = activate(first_behind[..., :channels], norm_gain).astype(jnp.bfloat16)
    extended = jnp.concatenate([previous, activated])
    first_frame = lax.axis_index("tm") * frames
    tap_mask = make_mask(clip_ids[0], first_frame, frames)
    patches = extract(extended, tap_mask)
    conv_rows = jnp.dot(patches, conv_weight, preferred_element_type=jnp.float32).astype(
        jnp.bfloat16
    )
    cotangent_rows = out_cotangent[0].reshape(-1, outputs)
    patch_grad = jnp.dot(cotangent_rows, conv_weight.T, preferred_element_type=jnp.float32)
    unused, pull_patch = jax.vjp(
        lambda field: extract(field, tap_mask), extended.astype(jnp.float32)
    )
    extended_grad = pull_patch(patch_grad)[0]
    returned = from_behind(extended_grad[:2], "tm", -1)
    own_grad = extended_grad[2:] + returned
    unused, pull_norm = jax.vjp(lambda field: activate(field, norm_gain), video.astype(jnp.float32))
    video_grad = pull_norm(own_grad)[0].astype(jnp.bfloat16)
    chain_len = lax.axis_size("tm")
    scale = 1.0 / math.sqrt(lax.axis_size("dp") * chain_len * frames * height * width)
    kernel_rows = patches.shape[1]
    slab_rows = kernel_rows // chain_len
    slab_start = lax.axis_index("tm") * slab_rows
    tap_lo = slab_start // channels
    slab_offset = slab_start - tap_lo * channels
    group_both = ring_gather(both, "tm", first_behind)
    group_video = activate(group_both[..., :channels], norm_gain).astype(jnp.bfloat16)
    group_cot = group_both[..., channels:]
    group_frames = group_video.shape[0]
    group_mask = make_mask(clip_ids[0], 0, group_frames).astype(jnp.bfloat16)
    group_pad = jnp.pad(group_video, ((2, 0), (1, 1), (1, 1), (0, 0)))
    tap_count = -(-(slab_rows + channels - 1) // channels)
    columns = []
    for step in range(tap_count):
        tap = jnp.minimum(tap_lo + step, 26)
        tap_t, tap_h, tap_w = (tap // 9, tap // 3 % 3, tap % 3)
        window = lax.dynamic_slice(
            group_pad, (tap_t, tap_h, tap_w, 0), (group_frames, height, width, channels)
        )
        weight_t = lax.dynamic_index_in_dim(group_mask, tap_t, 1, keepdims=False)
        columns.append((window * weight_t[:, None, None, None]).reshape(-1, channels))
    slab_patches = lax.dynamic_slice_in_dim(jnp.concatenate(columns, axis=1), slab_offset, slab_rows, 1)
    slab_t = lax.dot_general(
        group_cot.reshape(-1, outputs),
        slab_patches,
        (((0,), (0,)), ((), ())),
        preferred_element_type=jnp.float32,
    )
    groups = lax.axis_size("dp")
    pieces = slab_t.reshape(groups, outputs // groups, slab_rows)
    reduced_t = lax.all_to_all(pieces, "dp", 0, 0, tiled=False).sum(axis=0)
    grad_weight = reduced_t.T * scale
    conv_out = conv_rows.reshape(1, frames, height, width, outputs)
    return (conv_out, video_grad[None], grad_weight)


def solution(mesh):
    in_specs = (
        P("dp", "tm", None, None, None),
        P("dp", None),
        P(),
        P(),
        P("dp", "tm", None, None, None),
    )
    out_specs = (P("dp", "tm", None, None, None), P("dp", "tm", None, None, None), P("tm", "dp"))
    return jax.shard_map(shards, mesh=mesh, in_specs=in_specs, out_specs=out_specs, check_vma=False)
```

```python
import math

import jax
import jax.numpy as jnp
from jax import lax
from jax.sharding import Mesh, PartitionSpec as P

DATA = ("dq", "dc")


def from_behind(block, axis, distance):
    devices = range(lax.axis_size(axis))
    route = [(i - distance, i) for i in devices if i - distance in devices]
    return lax.ppermute(block, axis, route)


def ring_route(axis, step):
    size = lax.axis_size(axis)
    return [(i, (i + step) % size) for i in range(size)]


def ring_gather(block, axis, first_behind):
    size = lax.axis_size(axis)
    from_ahead = []
    from_behind_list = [first_behind]
    for unused in range(size // 2 - 1):
        from_behind_list.append(lax.ppermute(from_behind_list[-1], axis, ring_route(axis, 1)))
    moving = block
    for unused in range(size - 1 - size // 2):
        moving = lax.ppermute(moving, axis, ring_route(axis, -1))
        from_ahead.append(moving)
    relative = [block] + from_ahead + from_behind_list[::-1]
    stacked = jnp.stack(relative, axis=0)
    ordered = jnp.roll(stacked, lax.axis_index(axis), axis=0)
    return ordered.reshape((-1,) + block.shape[1:])


def activate(video, norm_gain):
    values = video.astype(jnp.float32)
    mean_square = jnp.mean(values * values, axis=-1, keepdims=True)
    normed = values * lax.rsqrt(mean_square + 1e-06) * norm_gain
    return jax.nn.silu(normed)


def make_mask(clips, first_frame, count):
    padded_ids = jnp.concatenate([jnp.full((2,), -1, jnp.int32), clips])
    window = lax.dynamic_slice_in_dim(padded_ids, first_frame, count + 2)
    offsets = jnp.arange(count)[:, None] + jnp.arange(3)[None, :]
    current = window[jnp.arange(count) + 2][:, None]
    return (window[offsets] == current).astype(jnp.float32)


def extract(extended, tap_mask):
    frames = tap_mask.shape[0]
    height, width = (extended.shape[1], extended.shape[2])
    padded = jnp.pad(extended, ((0, 0), (1, 1), (1, 1), (0, 0)))
    taps = []
    for tap_t in range(3):
        weight_t = tap_mask[:, tap_t][:, None, None, None].astype(extended.dtype)
        for tap_h in range(3):
            for tap_w in range(3):
                taps.append(
                    padded[tap_t : tap_t + frames, tap_h : tap_h + height, tap_w : tap_w + width]
                    * weight_t
                )
    stacked = jnp.stack(taps, axis=3)
    return stacked.reshape(frames * height * width, -1)


def shards(clip_video, clip_ids, norm_gain, conv_weight, out_cotangent):
    video = clip_video[0]
    frames, height, width, channels = video.shape
    outputs = conv_weight.shape[1]
    activated = activate(video, norm_gain).astype(jnp.bfloat16)
    both = jnp.concatenate([video, out_cotangent[0]], axis=-1)
    first_behind = lax.ppermute(both, "tm", ring_route("tm", 1))
    previous = activate(first_behind[..., :channels], norm_gain).astype(jnp.bfloat16)
    extended = jnp.concatenate([previous, activated])
    first_frame = lax.axis_index("tm") * frames
    tap_mask = make_mask(clip_ids[0], first_frame, frames)
    patches = extract(extended, tap_mask)
    conv_rows = jnp.dot(patches, conv_weight, preferred_element_type=jnp.float32).astype(
        jnp.bfloat16
    )
    cotangent_rows = out_cotangent[0].reshape(-1, outputs)
    patch_grad = jnp.dot(cotangent_rows, conv_weight.T, preferred_element_type=jnp.float32)
    unused, pull_patch = jax.vjp(
        lambda field: extract(field, tap_mask), extended.astype(jnp.float32)
    )
    extended_grad = pull_patch(patch_grad)[0]
    returned = from_behind(extended_grad[:2], "tm", -1)
    own_grad = extended_grad[2:] + returned
    unused, pull_norm = jax.vjp(lambda field: activate(field, norm_gain), video.astype(jnp.float32))
    video_grad = pull_norm(own_grad)[0].astype(jnp.bfloat16)
    chain_len = lax.axis_size("tm")
    scale = 1.0 / math.sqrt(lax.axis_size(DATA) * chain_len * frames * height * width)
    kernel_rows = patches.shape[1]
    slab_rows = kernel_rows // chain_len
    slab_start = lax.axis_index("tm") * slab_rows
    tap_lo = slab_start // channels
    slab_offset = slab_start - tap_lo * channels
    group_both = ring_gather(both, "tm", first_behind)
    group_video = activate(group_both[..., :channels], norm_gain).astype(jnp.bfloat16)
    group_cot = group_both[..., channels:]
    group_frames = group_video.shape[0]
    group_mask = make_mask(clip_ids[0], 0, group_frames).astype(jnp.bfloat16)
    group_pad = jnp.pad(group_video, ((2, 0), (1, 1), (1, 1), (0, 0)))
    tap_count = -(-(slab_rows + channels - 1) // channels)
    columns = []
    for step in range(tap_count):
        tap = jnp.minimum(tap_lo + step, 26)
        tap_t, tap_h, tap_w = (tap // 9, tap // 3 % 3, tap % 3)
        window = lax.dynamic_slice(
            group_pad, (tap_t, tap_h, tap_w, 0), (group_frames, height, width, channels)
        )
        weight_t = lax.dynamic_index_in_dim(group_mask, tap_t, 1, keepdims=False)
        columns.append((window * weight_t[:, None, None, None]).reshape(-1, channels))
    slab_patches = lax.dynamic_slice_in_dim(jnp.concatenate(columns, axis=1), slab_offset, slab_rows, 1)
    slab_t = lax.dot_general(
        group_cot.reshape(-1, outputs),
        slab_patches,
        (((0,), (0,)), ((), ())),
        preferred_element_type=jnp.float32,
    )
    chips = lax.axis_size("dq")
    cores = lax.axis_size("dc")
    pieces = slab_t.reshape(chips, cores, outputs // (chips * cores), slab_rows)
    core = lax.axis_index("dc")
    kept = lax.dynamic_index_in_dim(pieces, core, 1, keepdims=False)
    sent = lax.dynamic_index_in_dim(pieces, 1 - core, 1, keepdims=False)
    pair_sum = kept + lax.ppermute(sent, "dc", [(0, 1), (1, 0)])
    reduced_t = lax.all_to_all(pair_sum, "dq", 0, 0, tiled=False).sum(axis=0)
    grad_weight = reduced_t.T * scale
    conv_out = conv_rows.reshape(1, frames, height, width, outputs)
    return (conv_out, video_grad[None], grad_weight)


def solution(mesh):
    devices = mesh.devices.reshape(mesh.shape["tm"], -1, 2)
    split_mesh = Mesh(devices, ("tm", "dq", "dc"))
    in_specs = (
        P(DATA, "tm", None, None, None),
        P(DATA, None),
        P(),
        P(),
        P(DATA, "tm", None, None, None),
    )
    out_specs = (
        P(DATA, "tm", None, None, None),
        P(DATA, "tm", None, None, None),
        P("tm", DATA),
    )
    return jax.shard_map(
        shards, mesh=split_mesh, in_specs=in_specs, out_specs=out_specs, check_vma=False
    )
```

```python
import math

import jax
import jax.numpy as jnp
from jax import lax
from jax.sharding import Mesh, PartitionSpec as P

DATA = ("dq", "dc")


def from_behind(block, axis, distance):
    devices = range(lax.axis_size(axis))
    route = [(i - distance, i) for i in devices if i - distance in devices]
    return lax.ppermute(block, axis, route)


def ring_route(axis, step):
    size = lax.axis_size(axis)
    return [(i, (i + step) % size) for i in range(size)]


def ring_gather(block, axis, first_behind):
    size = lax.axis_size(axis)
    from_ahead = []
    from_behind_list = [first_behind]
    for unused in range(size // 2 - 1):
        from_behind_list.append(lax.ppermute(from_behind_list[-1], axis, ring_route(axis, 1)))
    moving = block
    for unused in range(size - 1 - size // 2):
        moving = lax.ppermute(moving, axis, ring_route(axis, -1))
        from_ahead.append(moving)
    relative = [block] + from_ahead + from_behind_list[::-1]
    stacked = jnp.stack(relative, axis=0)
    ordered = jnp.roll(stacked, lax.axis_index(axis), axis=0)
    return ordered.reshape((-1,) + block.shape[1:])


def activate(video, norm_gain):
    values = video.astype(jnp.float32)
    mean_square = jnp.mean(values * values, axis=-1, keepdims=True)
    normed = values * lax.rsqrt(mean_square + 1e-06) * norm_gain
    return jax.nn.silu(normed)


def make_mask(clips, first_frame, count):
    padded_ids = jnp.concatenate([jnp.full((2,), -1, jnp.int32), clips])
    window = lax.dynamic_slice_in_dim(padded_ids, first_frame, count + 2)
    offsets = jnp.arange(count)[:, None] + jnp.arange(3)[None, :]
    current = window[jnp.arange(count) + 2][:, None]
    return (window[offsets] == current).astype(jnp.float32)


def extract(extended, tap_mask):
    frames = tap_mask.shape[0]
    height, width = (extended.shape[1], extended.shape[2])
    padded = jnp.pad(extended, ((0, 0), (1, 1), (1, 1), (0, 0)))
    taps = []
    for tap_t in range(3):
        weight_t = tap_mask[:, tap_t][:, None, None, None].astype(extended.dtype)
        for tap_h in range(3):
            for tap_w in range(3):
                taps.append(
                    padded[tap_t : tap_t + frames, tap_h : tap_h + height, tap_w : tap_w + width]
                    * weight_t
                )
    stacked = jnp.stack(taps, axis=3)
    return stacked.reshape(frames * height * width, -1)


def shards(clip_video, clip_ids, norm_gain, conv_weight, out_cotangent):
    video = clip_video[0]
    frames, height, width, channels = video.shape
    outputs = conv_weight.shape[1]
    activated = activate(video, norm_gain).astype(jnp.bfloat16)
    both = jnp.concatenate([video, out_cotangent[0]], axis=-1)
    first_behind = lax.ppermute(both, "tm", ring_route("tm", 1))
    previous = activate(first_behind[..., :channels], norm_gain).astype(jnp.bfloat16)
    extended = jnp.concatenate([previous, activated])
    first_frame = lax.axis_index("tm") * frames
    tap_mask = make_mask(clip_ids[0], first_frame, frames)
    kernel = conv_weight.reshape(3, 3, 3, channels, outputs)
    tap_scale = tap_mask[:, :, None, None, None]
    taps = jnp.stack([extended[tap_t : tap_t + frames] for tap_t in range(3)], axis=1)
    masked_taps = taps * tap_scale.astype(taps.dtype)
    conv_rows = lax.conv_general_dilated(
        masked_taps,
        kernel,
        (1, 1, 1),
        ((0, 0), (1, 1), (1, 1)),
        dimension_numbers=("NDHWC", "DHWIO", "NDHWC"),
        preferred_element_type=jnp.float32,
    ).astype(jnp.bfloat16)
    taps_grad = lax.conv_general_dilated(
        out_cotangent[0][:, None],
        kernel[::-1, ::-1, ::-1],
        (1, 1, 1),
        ((2, 2), (1, 1), (1, 1)),
        dimension_numbers=("NDHWC", "DHWOI", "NDHWC"),
        preferred_element_type=jnp.float32,
    )
    masked_grad = taps_grad * tap_scale
    extended_grad = sum(
        jnp.pad(masked_grad[:, tap_t], ((tap_t, 2 - tap_t), (0, 0), (0, 0), (0, 0)))
        for tap_t in range(3)
    )
    returned = from_behind(extended_grad[:2], "tm", -1)
    own_grad = extended_grad[2:] + returned
    unused, pull_norm = jax.vjp(lambda field: activate(field, norm_gain), video.astype(jnp.float32))
    video_grad = pull_norm(own_grad)[0].astype(jnp.bfloat16)
    chain_len = lax.axis_size("tm")
    scale = 1.0 / math.sqrt(lax.axis_size(DATA) * chain_len * frames * height * width)
    kernel_rows = conv_weight.shape[0]
    slab_rows = kernel_rows // chain_len
    slab_start = lax.axis_index("tm") * slab_rows
    tap_lo = slab_start // channels
    slab_offset = slab_start - tap_lo * channels
    group_both = ring_gather(both, "tm", first_behind)
    group_video = activate(group_both[..., :channels], norm_gain).astype(jnp.bfloat16)
    group_cot = group_both[..., channels:]
    group_frames = group_video.shape[0]
    group_mask = make_mask(clip_ids[0], 0, group_frames).astype(jnp.bfloat16)
    group_pad = jnp.pad(group_video, ((2, 0), (1, 1), (1, 1), (0, 0)))
    tap_count = -(-(slab_rows + channels - 1) // channels)
    columns = []
    for step in range(tap_count):
        tap = jnp.minimum(tap_lo + step, 26)
        tap_t, tap_h, tap_w = (tap // 9, tap // 3 % 3, tap % 3)
        window = lax.dynamic_slice(
            group_pad, (tap_t, tap_h, tap_w, 0), (group_frames, height, width, channels)
        )
        weight_t = lax.dynamic_index_in_dim(group_mask, tap_t, 1, keepdims=False)
        columns.append((window * weight_t[:, None, None, None]).reshape(-1, channels))
    slab_patches = lax.dynamic_slice_in_dim(jnp.concatenate(columns, axis=1), slab_offset, slab_rows, 1)
    slab_t = lax.dot_general(
        group_cot.reshape(-1, outputs),
        slab_patches,
        (((0,), (0,)), ((), ())),
        preferred_element_type=jnp.float32,
    )
    chips = lax.axis_size("dq")
    cores = lax.axis_size("dc")
    pieces = slab_t.reshape(chips, cores, outputs // (chips * cores), slab_rows)
    core = lax.axis_index("dc")
    kept = lax.dynamic_index_in_dim(pieces, core, 1, keepdims=False)
    sent = lax.dynamic_index_in_dim(pieces, 1 - core, 1, keepdims=False)
    pair_sum = kept + lax.ppermute(sent, "dc", [(0, 1), (1, 0)])
    reduced_t = lax.all_to_all(pair_sum, "dq", 0, 0, tiled=False).sum(axis=0)
    grad_weight = reduced_t.T * scale
    conv_out = conv_rows.reshape(1, frames, height, width, outputs)
    return (conv_out, video_grad[None], grad_weight)


def solution(mesh):
    devices = mesh.devices.reshape(mesh.shape["tm"], -1, 2)
    split_mesh = Mesh(devices, ("tm", "dq", "dc"))
    in_specs = (
        P(DATA, "tm", None, None, None),
        P(DATA, None),
        P(),
        P(),
        P(DATA, "tm", None, None, None),
    )
    out_specs = (
        P(DATA, "tm", None, None, None),
        P(DATA, "tm", None, None, None),
        P("tm", DATA),
    )
    return jax.shard_map(
        shards, mesh=split_mesh, in_specs=in_specs, out_specs=out_specs, check_vma=False
    )
```

```python
import math

import jax
import jax.numpy as jnp
from jax import lax
from jax.sharding import Mesh, PartitionSpec as P

DATA = ("dq", "dc")


def from_behind(block, axis, distance):
    devices = range(lax.axis_size(axis))
    route = [(i - distance, i) for i in devices if i - distance in devices]
    return lax.ppermute(block, axis, route)


def ring_route(axis, step):
    size = lax.axis_size(axis)
    return [(i, (i + step) % size) for i in range(size)]


def ring_blocks(block, axis, first_behind):
    size = lax.axis_size(axis)
    relative = [None] * size
    relative[0] = block
    relative[size - 1] = first_behind
    moving = first_behind
    for step in range(2, size // 2 + 1):
        moving = lax.ppermute(moving, axis, ring_route(axis, 1))
        relative[size - step] = moving
    moving = block
    for step in range(1, size - size // 2):
        moving = lax.ppermute(moving, axis, ring_route(axis, -1))
        relative[step] = moving
    return relative


def activate(video, norm_gain):
    values = video.astype(jnp.float32)
    mean_square = jnp.mean(values * values, axis=-1, keepdims=True)
    normed = values * lax.rsqrt(mean_square + 1e-06) * norm_gain
    return jax.nn.silu(normed)


def make_mask(clips, first_frame, count):
    padded_ids = jnp.concatenate([jnp.full((2,), -1, jnp.int32), clips])
    window = lax.dynamic_slice_in_dim(padded_ids, first_frame, count + 2)
    offsets = jnp.arange(count)[:, None] + jnp.arange(3)[None, :]
    current = window[jnp.arange(count) + 2][:, None]
    return (window[offsets] == current).astype(jnp.float32)


def extract(extended, tap_mask):
    frames = tap_mask.shape[0]
    height, width = (extended.shape[1], extended.shape[2])
    padded = jnp.pad(extended, ((0, 0), (1, 1), (1, 1), (0, 0)))
    taps = []
    for tap_t in range(3):
        weight_t = tap_mask[:, tap_t][:, None, None, None].astype(extended.dtype)
        for tap_h in range(3):
            for tap_w in range(3):
                taps.append(
                    padded[tap_t : tap_t + frames, tap_h : tap_h + height, tap_w : tap_w + width]
                    * weight_t
                )
    stacked = jnp.stack(taps, axis=3)
    return stacked.reshape(frames * height * width, -1)


def shards(clip_video, clip_ids, norm_gain, conv_weight, out_cotangent):
    video = clip_video[0]
    frames, height, width, channels = video.shape
    outputs = conv_weight.shape[1]
    activated = activate(video, norm_gain).astype(jnp.bfloat16)
    both = jnp.concatenate([video, out_cotangent[0]], axis=-1)
    first_behind = lax.ppermute(both, "tm", ring_route("tm", 1))
    previous = activate(first_behind[..., :channels], norm_gain).astype(jnp.bfloat16)
    extended = jnp.concatenate([previous, activated])
    first_frame = lax.axis_index("tm") * frames
    tap_mask = make_mask(clip_ids[0], first_frame, frames)
    kernel = conv_weight.reshape(3, 3, 3, channels, outputs)
    tap_scale = tap_mask[:, :, None, None, None]
    taps = jnp.stack([extended[tap_t : tap_t + frames] for tap_t in range(3)], axis=1)
    masked_taps = taps * tap_scale.astype(taps.dtype)
    conv_rows = lax.conv_general_dilated(
        masked_taps,
        kernel,
        (1, 1, 1),
        ((0, 0), (1, 1), (1, 1)),
        dimension_numbers=("NDHWC", "DHWIO", "NDHWC"),
        preferred_element_type=jnp.float32,
    ).astype(jnp.bfloat16)
    taps_grad = lax.conv_general_dilated(
        out_cotangent[0][:, None],
        kernel[::-1, ::-1, ::-1],
        (1, 1, 1),
        ((2, 2), (1, 1), (1, 1)),
        dimension_numbers=("NDHWC", "DHWOI", "NDHWC"),
        preferred_element_type=jnp.float32,
    )
    masked_grad = taps_grad * tap_scale
    extended_grad = sum(
        jnp.pad(masked_grad[:, tap_t], ((tap_t, 2 - tap_t), (0, 0), (0, 0), (0, 0)))
        for tap_t in range(3)
    )
    returned = from_behind(extended_grad[:2], "tm", -1)
    own_grad = extended_grad[2:] + returned
    unused, pull_norm = jax.vjp(lambda field: activate(field, norm_gain), video.astype(jnp.float32))
    video_grad = pull_norm(own_grad)[0].astype(jnp.bfloat16)
    chain_len = lax.axis_size("tm")
    scale = 1.0 / math.sqrt(lax.axis_size(DATA) * chain_len * frames * height * width)
    kernel_rows = conv_weight.shape[0]
    slab_rows = kernel_rows // chain_len
    slab_start = lax.axis_index("tm") * slab_rows
    tap_lo = slab_start // channels
    slab_offset = slab_start - tap_lo * channels
    blocks = ring_blocks(both, "tm", first_behind)
    block_acts = [activated] + [
        activate(block[..., :channels], norm_gain).astype(jnp.bfloat16) for block in blocks[1:-1]
    ] + [previous]
    group_mask = make_mask(clip_ids[0], 0, frames * chain_len).astype(jnp.bfloat16)
    tap_count = -(-(slab_rows + channels - 1) // channels)
    tap_params = []
    for step in range(tap_count):
        tap = jnp.minimum(tap_lo + step, 26)
        tap_params.append((tap // 9, tap // 3 % 3, tap % 3))
    me = lax.axis_index("tm")
    total = None
    for rel in range(chain_len):
        ext_pad = jnp.pad(
            jnp.concatenate([block_acts[rel - 1], block_acts[rel]]),
            ((0, 0), (1, 1), (1, 1), (0, 0)),
        )
        owner = (me + rel) % chain_len
        block_mask = lax.dynamic_slice_in_dim(group_mask, owner * frames, frames, 0)
        columns = []
        for tap_t, tap_h, tap_w in tap_params:
            window = lax.dynamic_slice(
                ext_pad, (tap_t, tap_h, tap_w, 0), (frames, height, width, channels)
            )
            weight_t = lax.dynamic_index_in_dim(block_mask, tap_t, 1, keepdims=False)
            columns.append((window * weight_t[:, None, None, None]).reshape(-1, channels))
        block_cot = blocks[rel][..., channels:].reshape(-1, outputs)
        term = lax.dot_general(
            block_cot,
            jnp.concatenate(columns, axis=1),
            (((0,), (0,)), ((), ())),
            preferred_element_type=jnp.float32,
        )
        total = term if total is None else total + term
    slab_t = lax.dynamic_slice_in_dim(total, slab_offset, slab_rows, 1)
    chips = lax.axis_size("dq")
    cores = lax.axis_size("dc")
    pieces = slab_t.reshape(chips, cores, outputs // (chips * cores), slab_rows)
    core = lax.axis_index("dc")
    kept = lax.dynamic_index_in_dim(pieces, core, 1, keepdims=False)
    sent = lax.dynamic_index_in_dim(pieces, 1 - core, 1, keepdims=False)
    pair_sum = kept + lax.ppermute(sent, "dc", [(0, 1), (1, 0)])
    reduced_t = lax.all_to_all(pair_sum, "dq", 0, 0, tiled=False).sum(axis=0)
    grad_weight = reduced_t.T * scale
    conv_out = conv_rows.reshape(1, frames, height, width, outputs)
    return (conv_out, video_grad[None], grad_weight)


def solution(mesh):
    devices = mesh.devices.reshape(mesh.shape["tm"], -1, 2)
    split_mesh = Mesh(devices, ("tm", "dq", "dc"))
    in_specs = (
        P(DATA, "tm", None, None, None),
        P(DATA, None),
        P(),
        P(),
        P(DATA, "tm", None, None, None),
    )
    out_specs = (
        P(DATA, "tm", None, None, None),
        P(DATA, "tm", None, None, None),
        P("tm", DATA),
    )
    return jax.shard_map(
        shards, mesh=split_mesh, in_specs=in_specs, out_specs=out_specs, check_vma=False
    )
```

```python
import math

import jax
import jax.numpy as jnp
from jax import lax
from jax.sharding import Mesh, PartitionSpec as P

DATA = ("dq", "dc")


def from_behind(block, axis, distance):
    devices = range(lax.axis_size(axis))
    route = [(i - distance, i) for i in devices if i - distance in devices]
    return lax.ppermute(block, axis, route)


def ring_route(axis, step):
    size = lax.axis_size(axis)
    return [(i, (i + step) % size) for i in range(size)]


def ring_blocks(block, axis, first_behind):
    size = lax.axis_size(axis)
    relative = [None] * size
    relative[0] = block
    relative[size - 1] = first_behind
    moving = first_behind
    for step in range(2, size // 2 + 1):
        moving = lax.ppermute(moving, axis, ring_route(axis, 1))
        relative[size - step] = moving
    moving = block
    for step in range(1, size - size // 2):
        moving = lax.ppermute(moving, axis, ring_route(axis, -1))
        relative[step] = moving
    return relative


def activate(video, norm_gain):
    values = video.astype(jnp.float32)
    mean_square = jnp.mean(values * values, axis=-1, keepdims=True)
    normed = values * lax.rsqrt(mean_square + 1e-06) * norm_gain
    return jax.nn.silu(normed)


def make_mask(clips, first_frame, count):
    padded_ids = jnp.concatenate([jnp.full((2,), -1, jnp.int32), clips])
    window = lax.dynamic_slice_in_dim(padded_ids, first_frame, count + 2)
    offsets = jnp.arange(count)[:, None] + jnp.arange(3)[None, :]
    current = window[jnp.arange(count) + 2][:, None]
    return (window[offsets] == current).astype(jnp.float32)


def extract(extended, tap_mask):
    frames = tap_mask.shape[0]
    height, width = (extended.shape[1], extended.shape[2])
    padded = jnp.pad(extended, ((0, 0), (1, 1), (1, 1), (0, 0)))
    taps = []
    for tap_t in range(3):
        weight_t = tap_mask[:, tap_t][:, None, None, None].astype(extended.dtype)
        for tap_h in range(3):
            for tap_w in range(3):
                taps.append(
                    padded[tap_t : tap_t + frames, tap_h : tap_h + height, tap_w : tap_w + width]
                    * weight_t
                )
    stacked = jnp.stack(taps, axis=3)
    return stacked.reshape(frames * height * width, -1)


def shards(clip_video, clip_ids, norm_gain, conv_weight, out_cotangent):
    video = clip_video[0]
    frames, height, width, channels = video.shape
    outputs = conv_weight.shape[1]
    activated = activate(video, norm_gain).astype(jnp.bfloat16)
    both = jnp.concatenate([video, out_cotangent[0]], axis=-1)
    first_behind = lax.ppermute(both, "tm", ring_route("tm", 1))
    previous = activate(first_behind[..., :channels], norm_gain).astype(jnp.bfloat16)
    extended = jnp.concatenate([previous, activated])
    first_frame = lax.axis_index("tm") * frames
    tap_mask = make_mask(clip_ids[0], first_frame, frames)
    kernel = conv_weight.reshape(3, 3, 3, channels, outputs)
    tap_scale = tap_mask[:, :, None, None, None]
    taps = jnp.stack([extended[tap_t : tap_t + frames] for tap_t in range(3)], axis=1)
    masked_taps = taps * tap_scale.astype(taps.dtype)
    conv_rows = lax.conv_general_dilated(
        masked_taps,
        kernel,
        (1, 1, 1),
        ((0, 0), (1, 1), (1, 1)),
        dimension_numbers=("NDHWC", "DHWIO", "NDHWC"),
        preferred_element_type=jnp.float32,
    ).astype(jnp.bfloat16)
    taps_grad = lax.conv_general_dilated(
        out_cotangent[0][:, None],
        kernel[::-1, ::-1, ::-1],
        (1, 1, 1),
        ((2, 2), (1, 1), (1, 1)),
        dimension_numbers=("NDHWC", "DHWOI", "NDHWC"),
        preferred_element_type=jnp.float32,
    )
    masked_grad = taps_grad * tap_scale
    extended_grad = sum(
        jnp.pad(masked_grad[:, tap_t], ((tap_t, 2 - tap_t), (0, 0), (0, 0), (0, 0)))
        for tap_t in range(3)
    )
    returned = from_behind(extended_grad[:2], "tm", -1)
    own_grad = extended_grad[2:] + returned
    unused, pull_norm = jax.vjp(lambda field: activate(field, norm_gain), video.astype(jnp.float32))
    video_grad = pull_norm(own_grad)[0].astype(jnp.bfloat16)
    chain_len = lax.axis_size("tm")
    scale = 1.0 / math.sqrt(lax.axis_size(DATA) * chain_len * frames * height * width)
    kernel_rows = conv_weight.shape[0]
    slab_rows = kernel_rows // chain_len
    slab_start = lax.axis_index("tm") * slab_rows
    tap_lo = slab_start // channels
    slab_offset = slab_start - tap_lo * channels
    group_mask = make_mask(clip_ids[0], 0, frames * chain_len).astype(jnp.bfloat16)
    tap_count = max(
        -(-(slab_rows * index % channels + slab_rows) // channels) for index in range(chain_len)
    )
    tap_params = []
    for step in range(tap_count):
        tap = jnp.minimum(tap_lo + step, 26)
        tap_params.append((tap // 9, tap // 3 % 3, tap % 3))
    me = lax.axis_index("tm")
    blocks = [None] * chain_len
    block_acts = [None] * chain_len
    blocks[0], block_acts[0] = both, activated
    blocks[-1], block_acts[-1] = first_behind, previous

    def block_term(rel):
        ext_pad = jnp.pad(
            jnp.concatenate([block_acts[rel - 1], block_acts[rel]]),
            ((0, 0), (1, 1), (1, 1), (0, 0)),
        )
        owner = (me + rel) % chain_len
        block_mask = lax.dynamic_slice_in_dim(group_mask, owner * frames, frames, 0)
        columns = []
        for tap_t, tap_h, tap_w in tap_params:
            window = lax.dynamic_slice(
                ext_pad, (tap_t, tap_h, tap_w, 0), (frames, height, width, channels)
            )
            weight_t = lax.dynamic_index_in_dim(block_mask, tap_t, 1, keepdims=False)
            columns.append((window * weight_t[:, None, None, None]).reshape(-1, channels))
        block_cot = blocks[rel][..., channels:].reshape(-1, outputs)
        return lax.dot_general(
            block_cot,
            jnp.concatenate(columns, axis=1),
            (((0,), (0,)), ((), ())),
            preferred_element_type=jnp.float32,
        )

    pending = list(range(chain_len))

    def add_ready(total):
        for rel in list(pending):
            if block_acts[rel] is not None and block_acts[rel - 1] is not None:
                term = block_term(rel)
                total = term if total is None else total + term
                pending.remove(rel)
        return total

    total = None
    forward_steps = chain_len // 2
    backward_steps = chain_len - 1 - forward_steps
    forward_moving = first_behind
    backward_moving = lax.ppermute(both, "tm", ring_route("tm", -1))
    arrived = [(chain_len - 1, None), (1, backward_moving)]
    for step in range(2, forward_steps + 1):
        total = add_ready(total)
        if total is not None:
            forward_moving, backward_moving, total = lax.optimization_barrier(
                (forward_moving, backward_moving, total)
            )
        for rel, block in arrived:
            if block is not None:
                blocks[rel] = block
                block_acts[rel] = activate(block[..., :channels], norm_gain).astype(jnp.bfloat16)
        forward_moving = lax.ppermute(forward_moving, "tm", ring_route("tm", 1))
        arrived = [(chain_len - step, forward_moving)]
        if step <= backward_steps:
            backward_moving = lax.ppermute(backward_moving, "tm", ring_route("tm", -1))
            arrived.append((step, backward_moving))
    for rel, block in arrived:
        blocks[rel] = block
        block_acts[rel] = activate(block[..., :channels], norm_gain).astype(jnp.bfloat16)
    total = add_ready(total)
    slab_t = lax.dynamic_slice_in_dim(total, slab_offset, slab_rows, 1)
    chips = lax.axis_size("dq")
    cores = lax.axis_size("dc")
    pieces = slab_t.reshape(chips, cores, outputs // (chips * cores), slab_rows)
    core = lax.axis_index("dc")
    kept = lax.dynamic_index_in_dim(pieces, core, 1, keepdims=False)
    sent = lax.dynamic_index_in_dim(pieces, 1 - core, 1, keepdims=False)
    pair_sum = kept + lax.ppermute(sent, "dc", [(0, 1), (1, 0)])
    reduced_t = lax.all_to_all(pair_sum, "dq", 0, 0, tiled=False).sum(axis=0)
    grad_weight = reduced_t.T * scale
    conv_out = conv_rows.reshape(1, frames, height, width, outputs)
    return (conv_out, video_grad[None], grad_weight)


def solution(mesh):
    devices = mesh.devices.reshape(mesh.shape["tm"], -1, 2)
    split_mesh = Mesh(devices, ("tm", "dq", "dc"))
    in_specs = (
        P(DATA, "tm", None, None, None),
        P(DATA, None),
        P(),
        P(),
        P(DATA, "tm", None, None, None),
    )
    out_specs = (
        P(DATA, "tm", None, None, None),
        P(DATA, "tm", None, None, None),
        P("tm", DATA),
    )
    return jax.shard_map(
        shards, mesh=split_mesh, in_specs=in_specs, out_specs=out_specs, check_vma=False
    )
```

```python
import math

import jax
import jax.numpy as jnp
from jax import lax
from jax.sharding import Mesh, PartitionSpec as P

DATA = ("dq", "dc")


def from_behind(block, axis, distance):
    devices = range(lax.axis_size(axis))
    route = [(i - distance, i) for i in devices if i - distance in devices]
    return lax.ppermute(block, axis, route)


def ring_route(axis, step):
    size = lax.axis_size(axis)
    return [(i, (i + step) % size) for i in range(size)]


def ring_blocks(block, axis, first_behind):
    size = lax.axis_size(axis)
    relative = [None] * size
    relative[0] = block
    relative[size - 1] = first_behind
    moving = first_behind
    for step in range(2, size // 2 + 1):
        moving = lax.ppermute(moving, axis, ring_route(axis, 1))
        relative[size - step] = moving
    moving = block
    for step in range(1, size - size // 2):
        moving = lax.ppermute(moving, axis, ring_route(axis, -1))
        relative[step] = moving
    return relative


def activate(video, norm_gain):
    values = video.astype(jnp.float32)
    mean_square = jnp.mean(values * values, axis=-1, keepdims=True)
    normed = values * lax.rsqrt(mean_square + 1e-06) * norm_gain
    return jax.nn.silu(normed)


def make_mask(clips, first_frame, count):
    padded_ids = jnp.concatenate([jnp.full((2,), -1, jnp.int32), clips])
    window = lax.dynamic_slice_in_dim(padded_ids, first_frame, count + 2)
    offsets = jnp.arange(count)[:, None] + jnp.arange(3)[None, :]
    current = window[jnp.arange(count) + 2][:, None]
    return (window[offsets] == current).astype(jnp.float32)


def extract(extended, tap_mask):
    frames = tap_mask.shape[0]
    height, width = (extended.shape[1], extended.shape[2])
    padded = jnp.pad(extended, ((0, 0), (1, 1), (1, 1), (0, 0)))
    taps = []
    for tap_t in range(3):
        weight_t = tap_mask[:, tap_t][:, None, None, None].astype(extended.dtype)
        for tap_h in range(3):
            for tap_w in range(3):
                taps.append(
                    padded[tap_t : tap_t + frames, tap_h : tap_h + height, tap_w : tap_w + width]
                    * weight_t
                )
    stacked = jnp.stack(taps, axis=3)
    return stacked.reshape(frames * height * width, -1)


def shards(clip_video, clip_ids, norm_gain, conv_weight, out_cotangent):
    video = clip_video[0]
    frames, height, width, channels = video.shape
    outputs = conv_weight.shape[1]
    activated = activate(video, norm_gain).astype(jnp.bfloat16)
    both = jnp.concatenate([video, out_cotangent[0]], axis=-1)
    first_behind = lax.ppermute(both, "tm", ring_route("tm", 1))
    previous = activate(first_behind[..., :channels], norm_gain).astype(jnp.bfloat16)
    extended = jnp.concatenate([previous, activated])
    chain_len = lax.axis_size("tm")
    scale = 1.0 / math.sqrt(lax.axis_size(DATA) * chain_len * frames * height * width)
    kernel_rows = conv_weight.shape[0]
    slab_rows = kernel_rows // chain_len
    slab_start = lax.axis_index("tm") * slab_rows
    tap_lo = slab_start // channels
    slab_offset = slab_start - tap_lo * channels
    group_mask = make_mask(clip_ids[0], 0, frames * chain_len).astype(jnp.bfloat16)
    tap_count = max(
        -(-(slab_rows * index % channels + slab_rows) // channels) for index in range(chain_len)
    )
    tap_params = []
    for step in range(tap_count):
        tap = jnp.minimum(tap_lo + step, 26)
        tap_params.append((tap // 9, tap // 3 % 3, tap % 3))
    me = lax.axis_index("tm")
    blocks = [None] * chain_len
    block_acts = [None] * chain_len
    blocks[0], block_acts[0] = both, activated
    blocks[-1], block_acts[-1] = first_behind, previous

    def block_term(rel):
        ext_pad = jnp.pad(
            jnp.concatenate([block_acts[rel - 1], block_acts[rel]]),
            ((0, 0), (1, 1), (1, 1), (0, 0)),
        )
        owner = (me + rel) % chain_len
        block_mask = lax.dynamic_slice_in_dim(group_mask, owner * frames, frames, 0)
        columns = []
        for tap_t, tap_h, tap_w in tap_params:
            window = lax.dynamic_slice(
                ext_pad, (tap_t, tap_h, tap_w, 0), (frames, height, width, channels)
            )
            weight_t = lax.dynamic_index_in_dim(block_mask, tap_t, 1, keepdims=False)
            columns.append((window * weight_t[:, None, None, None]).reshape(-1, channels))
        block_cot = blocks[rel][..., channels:].reshape(-1, outputs)
        return lax.dot_general(
            block_cot,
            jnp.concatenate(columns, axis=1),
            (((0,), (0,)), ((), ())),
            preferred_element_type=jnp.float32,
        )

    def conv_section(extended, cotangent, conv_weight, video):
        first_frame = lax.axis_index("tm") * frames
        tap_mask = make_mask(clip_ids[0], first_frame, frames)
        kernel = conv_weight.reshape(3, 3, 3, channels, outputs)
        tap_scale = tap_mask[:, :, None, None, None]
        taps = jnp.stack([extended[tap_t : tap_t + frames] for tap_t in range(3)], axis=1)
        masked_taps = taps * tap_scale.astype(taps.dtype)
        conv_rows = lax.conv_general_dilated(
            masked_taps,
            kernel,
            (1, 1, 1),
            ((0, 0), (1, 1), (1, 1)),
            dimension_numbers=("NDHWC", "DHWIO", "NDHWC"),
            preferred_element_type=jnp.float32,
        ).astype(jnp.bfloat16)
        taps_grad = lax.conv_general_dilated(
            cotangent[:, None],
            kernel[::-1, ::-1, ::-1],
            (1, 1, 1),
            ((2, 2), (1, 1), (1, 1)),
            dimension_numbers=("NDHWC", "DHWOI", "NDHWC"),
            preferred_element_type=jnp.float32,
        )
        masked_grad = taps_grad * tap_scale
        extended_grad = sum(
            jnp.pad(masked_grad[:, tap_t], ((tap_t, 2 - tap_t), (0, 0), (0, 0), (0, 0)))
            for tap_t in range(3)
        )
        returned = from_behind(extended_grad[:2], "tm", -1)
        own_grad = extended_grad[2:] + returned
        unused, pull_norm = jax.vjp(lambda field: activate(field, norm_gain), video.astype(jnp.float32))
        video_grad = pull_norm(own_grad)[0].astype(jnp.bfloat16)
        return conv_rows, video_grad

    pending = list(range(chain_len))

    def add_ready(total):
        for rel in list(pending):
            if block_acts[rel] is not None and block_acts[rel - 1] is not None:
                term = block_term(rel)
                total = term if total is None else total + term
                pending.remove(rel)
        return total

    total = None
    conv_inputs = (extended, out_cotangent[0], conv_weight, video)
    forward_steps = chain_len // 2
    backward_steps = chain_len - 1 - forward_steps
    forward_moving = first_behind
    backward_moving = lax.ppermute(both, "tm", ring_route("tm", -1))
    arrived = [(chain_len - 1, None), (1, backward_moving)]
    for step in range(2, forward_steps + 1):
        total = add_ready(total)
        if step == 3:
            forward_moving, backward_moving, total, conv_inputs = lax.optimization_barrier(
                (forward_moving, backward_moving, total, conv_inputs)
            )
            conv_results = conv_section(*conv_inputs)
        elif step == 4:
            forward_moving, backward_moving, total, conv_results = lax.optimization_barrier(
                (forward_moving, backward_moving, total, conv_results)
            )
        elif total is not None:
            forward_moving, backward_moving, total = lax.optimization_barrier(
                (forward_moving, backward_moving, total)
            )
        for rel, block in arrived:
            if block is not None:
                blocks[rel] = block
                block_acts[rel] = activate(block[..., :channels], norm_gain).astype(jnp.bfloat16)
        forward_moving = lax.ppermute(forward_moving, "tm", ring_route("tm", 1))
        arrived = [(chain_len - step, forward_moving)]
        if step <= backward_steps:
            backward_moving = lax.ppermute(backward_moving, "tm", ring_route("tm", -1))
            arrived.append((step, backward_moving))
    for rel, block in arrived:
        blocks[rel] = block
        block_acts[rel] = activate(block[..., :channels], norm_gain).astype(jnp.bfloat16)
    total = add_ready(total)
    slab_t = lax.dynamic_slice_in_dim(total, slab_offset, slab_rows, 1)
    chips = lax.axis_size("dq")
    cores = lax.axis_size("dc")
    pieces = slab_t.reshape(chips, cores, outputs // (chips * cores), slab_rows)
    core = lax.axis_index("dc")
    kept = lax.dynamic_index_in_dim(pieces, core, 1, keepdims=False)
    sent = lax.dynamic_index_in_dim(pieces, 1 - core, 1, keepdims=False)
    pair_sum = kept + lax.ppermute(sent, "dc", [(0, 1), (1, 0)])
    conv_rows, video_grad = conv_results
    reduced_t = lax.all_to_all(pair_sum, "dq", 0, 0, tiled=False).sum(axis=0)
    grad_weight = reduced_t.T * scale
    conv_out = conv_rows.reshape(1, frames, height, width, outputs)
    return (conv_out, video_grad[None], grad_weight)


def solution(mesh):
    devices = mesh.devices.reshape(mesh.shape["tm"], -1, 2)
    split_mesh = Mesh(devices, ("tm", "dq", "dc"))
    in_specs = (
        P(DATA, "tm", None, None, None),
        P(DATA, None),
        P(),
        P(),
        P(DATA, "tm", None, None, None),
    )
    out_specs = (
        P(DATA, "tm", None, None, None),
        P(DATA, "tm", None, None, None),
        P("tm", DATA),
    )
    return jax.shard_map(
        shards, mesh=split_mesh, in_specs=in_specs, out_specs=out_specs, check_vma=False
    )
```

```python
import math

import jax
import jax.numpy as jnp
from jax import lax
from jax.sharding import Mesh, PartitionSpec as P

DATA = ("dq", "dc")


def from_behind(block, axis, distance):
    devices = range(lax.axis_size(axis))
    route = [(i - distance, i) for i in devices if i - distance in devices]
    return lax.ppermute(block, axis, route)


def ring_route(axis, step):
    size = lax.axis_size(axis)
    return [(i, (i + step) % size) for i in range(size)]


def ring_blocks(block, axis, first_behind):
    size = lax.axis_size(axis)
    relative = [None] * size
    relative[0] = block
    relative[size - 1] = first_behind
    moving = first_behind
    for step in range(2, size // 2 + 1):
        moving = lax.ppermute(moving, axis, ring_route(axis, 1))
        relative[size - step] = moving
    moving = block
    for step in range(1, size - size // 2):
        moving = lax.ppermute(moving, axis, ring_route(axis, -1))
        relative[step] = moving
    return relative


def activate(video, norm_gain):
    values = video.astype(jnp.float32)
    mean_square = jnp.mean(values * values, axis=-1, keepdims=True)
    normed = values * lax.rsqrt(mean_square + 1e-06) * norm_gain
    return jax.nn.silu(normed)


def make_mask(clips, first_frame, count):
    padded_ids = jnp.concatenate([jnp.full((2,), -1, jnp.int32), clips])
    window = lax.dynamic_slice_in_dim(padded_ids, first_frame, count + 2)
    offsets = jnp.arange(count)[:, None] + jnp.arange(3)[None, :]
    current = window[jnp.arange(count) + 2][:, None]
    return (window[offsets] == current).astype(jnp.float32)


def extract(extended, tap_mask):
    frames = tap_mask.shape[0]
    height, width = (extended.shape[1], extended.shape[2])
    padded = jnp.pad(extended, ((0, 0), (1, 1), (1, 1), (0, 0)))
    taps = []
    for tap_t in range(3):
        weight_t = tap_mask[:, tap_t][:, None, None, None].astype(extended.dtype)
        for tap_h in range(3):
            for tap_w in range(3):
                taps.append(
                    padded[tap_t : tap_t + frames, tap_h : tap_h + height, tap_w : tap_w + width]
                    * weight_t
                )
    stacked = jnp.stack(taps, axis=3)
    return stacked.reshape(frames * height * width, -1)


def shards(clip_video, clip_ids, norm_gain, conv_weight, out_cotangent):
    video = clip_video[0]
    frames, height, width, channels = video.shape
    outputs = conv_weight.shape[1]
    activated = activate(video, norm_gain).astype(jnp.bfloat16)
    both = jnp.concatenate([video, out_cotangent[0]], axis=-1)
    first_behind = lax.ppermute(both, "tm", ring_route("tm", 1))
    previous = activate(first_behind[..., :channels], norm_gain).astype(jnp.bfloat16)
    extended = jnp.concatenate([previous, activated])
    chain_len = lax.axis_size("tm")
    scale = 1.0 / math.sqrt(lax.axis_size(DATA) * chain_len * frames * height * width)
    kernel_rows = conv_weight.shape[0]
    slab_rows = kernel_rows // chain_len
    slab_start = lax.axis_index("tm") * slab_rows
    tap_lo = slab_start // channels
    slab_offset = slab_start - tap_lo * channels
    group_mask = make_mask(clip_ids[0], 0, frames * chain_len).astype(jnp.bfloat16)
    tap_count = max(
        -(-(slab_rows * index % channels + slab_rows) // channels) for index in range(chain_len)
    )
    tap_params = []
    for step in range(tap_count):
        tap = jnp.minimum(tap_lo + step, 26)
        tap_params.append((tap // 9, tap // 3 % 3, tap % 3))
    me = lax.axis_index("tm")
    blocks = [None] * chain_len
    block_acts = [None] * chain_len
    blocks[0], block_acts[0] = both, activated
    blocks[-1], block_acts[-1] = first_behind, previous

    def block_term(rel):
        ext_pad = jnp.pad(
            jnp.concatenate([block_acts[rel - 1], block_acts[rel]]),
            ((0, 0), (1, 1), (1, 1), (0, 0)),
        )
        owner = (me + rel) % chain_len
        block_mask = lax.dynamic_slice_in_dim(group_mask, owner * frames, frames, 0)
        columns = []
        for tap_t, tap_h, tap_w in tap_params:
            window = lax.dynamic_slice(
                ext_pad, (tap_t, tap_h, tap_w, 0), (frames, height, width, channels)
            )
            weight_t = lax.dynamic_index_in_dim(block_mask, tap_t, 1, keepdims=False)
            columns.append((window * weight_t[:, None, None, None]).reshape(-1, channels))
        block_cot = blocks[rel][..., channels:].reshape(-1, outputs)
        return lax.dot_general(
            block_cot,
            jnp.concatenate(columns, axis=1),
            (((0,), (0,)), ((), ())),
            preferred_element_type=jnp.float32,
        )

    def forward_section(extended, conv_weight):
        first_frame = lax.axis_index("tm") * frames
        tap_mask = make_mask(clip_ids[0], first_frame, frames)
        kernel = conv_weight.reshape(3, 3, 3, channels, outputs)
        tap_scale = tap_mask[:, :, None, None, None]
        taps = jnp.stack([extended[tap_t : tap_t + frames] for tap_t in range(3)], axis=1)
        masked_taps = taps * tap_scale.astype(taps.dtype)
        conv_rows = lax.conv_general_dilated(
            masked_taps,
            kernel,
            (1, 1, 1),
            ((0, 0), (1, 1), (1, 1)),
            dimension_numbers=("NDHWC", "DHWIO", "NDHWC"),
            preferred_element_type=jnp.float32,
        ).astype(jnp.bfloat16)
        return conv_rows

    def backward_section(cotangent, conv_weight, video):
        first_frame = lax.axis_index("tm") * frames
        tap_mask = make_mask(clip_ids[0], first_frame, frames)
        kernel = conv_weight.reshape(3, 3, 3, channels, outputs)
        tap_scale = tap_mask[:, :, None, None, None]
        taps_grad = lax.conv_general_dilated(
            cotangent[:, None],
            kernel[::-1, ::-1, ::-1],
            (1, 1, 1),
            ((2, 2), (1, 1), (1, 1)),
            dimension_numbers=("NDHWC", "DHWOI", "NDHWC"),
            preferred_element_type=jnp.float32,
        )
        masked_grad = taps_grad * tap_scale
        extended_grad = sum(
            jnp.pad(masked_grad[:, tap_t], ((tap_t, 2 - tap_t), (0, 0), (0, 0), (0, 0)))
            for tap_t in range(3)
        )
        returned = from_behind(extended_grad[:2], "tm", -1)
        own_grad = extended_grad[2:] + returned
        unused, pull_norm = jax.vjp(lambda field: activate(field, norm_gain), video.astype(jnp.float32))
        video_grad = pull_norm(own_grad)[0].astype(jnp.bfloat16)
        return video_grad

    pending = list(range(chain_len))

    def add_ready(total):
        for rel in list(pending):
            if block_acts[rel] is not None and block_acts[rel - 1] is not None:
                term = block_term(rel)
                total = term if total is None else total + term
                pending.remove(rel)
        return total

    total = None
    conv_inputs = (extended, conv_weight)
    grad_inputs = (out_cotangent[0], conv_weight, video)
    forward_steps = chain_len // 2
    backward_steps = chain_len - 1 - forward_steps
    forward_moving = first_behind
    backward_moving = lax.ppermute(both, "tm", ring_route("tm", -1))
    arrived = [(chain_len - 1, None), (1, backward_moving)]
    for step in range(2, forward_steps + 1):
        total = add_ready(total)
        if step == 3:
            forward_moving, backward_moving, total, conv_inputs = lax.optimization_barrier(
                (forward_moving, backward_moving, total, conv_inputs)
            )
            conv_rows = forward_section(*conv_inputs)
        elif step == 4:
            forward_moving, backward_moving, total, conv_rows, grad_inputs = (
                lax.optimization_barrier(
                    (forward_moving, backward_moving, total, conv_rows, grad_inputs)
                )
            )
        elif step == 5:
            forward_moving, backward_moving, total, grad_inputs = lax.optimization_barrier(
                (forward_moving, backward_moving, total, grad_inputs)
            )
            video_grad = backward_section(*grad_inputs)
        elif step == 6:
            forward_moving, backward_moving, total, video_grad = lax.optimization_barrier(
                (forward_moving, backward_moving, total, video_grad)
            )
        elif total is not None:
            forward_moving, backward_moving, total = lax.optimization_barrier(
                (forward_moving, backward_moving, total)
            )
        for rel, block in arrived:
            if block is not None:
                blocks[rel] = block
                block_acts[rel] = activate(block[..., :channels], norm_gain).astype(jnp.bfloat16)
        forward_moving = lax.ppermute(forward_moving, "tm", ring_route("tm", 1))
        arrived = [(chain_len - step, forward_moving)]
        if step <= backward_steps:
            backward_moving = lax.ppermute(backward_moving, "tm", ring_route("tm", -1))
            arrived.append((step, backward_moving))
    for rel, block in arrived:
        blocks[rel] = block
        block_acts[rel] = activate(block[..., :channels], norm_gain).astype(jnp.bfloat16)
    total = add_ready(total)
    slab_t = lax.dynamic_slice_in_dim(total, slab_offset, slab_rows, 1)
    chips = lax.axis_size("dq")
    cores = lax.axis_size("dc")
    pieces = slab_t.reshape(chips, cores, outputs // (chips * cores), slab_rows)
    core = lax.axis_index("dc")
    kept = lax.dynamic_index_in_dim(pieces, core, 1, keepdims=False)
    sent = lax.dynamic_index_in_dim(pieces, 1 - core, 1, keepdims=False)
    pair_sum = kept + lax.ppermute(sent, "dc", [(0, 1), (1, 0)])
    reduced_t = lax.all_to_all(pair_sum, "dq", 0, 0, tiled=False).sum(axis=0)
    grad_weight = reduced_t.T * scale
    conv_out = conv_rows.reshape(1, frames, height, width, outputs)
    return (conv_out, video_grad[None], grad_weight)


def solution(mesh):
    devices = mesh.devices.reshape(mesh.shape["tm"], -1, 2)
    split_mesh = Mesh(devices, ("tm", "dq", "dc"))
    in_specs = (
        P(DATA, "tm", None, None, None),
        P(DATA, None),
        P(),
        P(),
        P(DATA, "tm", None, None, None),
    )
    out_specs = (
        P(DATA, "tm", None, None, None),
        P(DATA, "tm", None, None, None),
        P("tm", DATA),
    )
    return jax.shard_map(
        shards, mesh=split_mesh, in_specs=in_specs, out_specs=out_specs, check_vma=False
    )
```

```python
import math

import jax
import jax.numpy as jnp
from jax import lax
from jax.sharding import Mesh, PartitionSpec as P

DATA = ("dq", "dc")


def from_behind(block, axis, distance):
    devices = range(lax.axis_size(axis))
    route = [(i - distance, i) for i in devices if i - distance in devices]
    return lax.ppermute(block, axis, route)


def ring_route(axis, step):
    size = lax.axis_size(axis)
    return [(i, (i + step) % size) for i in range(size)]


def ring_blocks(block, axis, first_behind):
    size = lax.axis_size(axis)
    relative = [None] * size
    relative[0] = block
    relative[size - 1] = first_behind
    moving = first_behind
    for step in range(2, size // 2 + 1):
        moving = lax.ppermute(moving, axis, ring_route(axis, 1))
        relative[size - step] = moving
    moving = block
    for step in range(1, size - size // 2):
        moving = lax.ppermute(moving, axis, ring_route(axis, -1))
        relative[step] = moving
    return relative


def activate(video, norm_gain):
    values = video.astype(jnp.float32)
    mean_square = jnp.mean(values * values, axis=-1, keepdims=True)
    normed = values * lax.rsqrt(mean_square + 1e-06) * norm_gain
    return jax.nn.silu(normed)


def make_mask(clips, first_frame, count):
    padded_ids = jnp.concatenate([jnp.full((2,), -1, jnp.int32), clips])
    window = lax.dynamic_slice_in_dim(padded_ids, first_frame, count + 2)
    offsets = jnp.arange(count)[:, None] + jnp.arange(3)[None, :]
    current = window[jnp.arange(count) + 2][:, None]
    return (window[offsets] == current).astype(jnp.float32)


def extract(extended, tap_mask):
    frames = tap_mask.shape[0]
    height, width = (extended.shape[1], extended.shape[2])
    padded = jnp.pad(extended, ((0, 0), (1, 1), (1, 1), (0, 0)))
    taps = []
    for tap_t in range(3):
        weight_t = tap_mask[:, tap_t][:, None, None, None].astype(extended.dtype)
        for tap_h in range(3):
            for tap_w in range(3):
                taps.append(
                    padded[tap_t : tap_t + frames, tap_h : tap_h + height, tap_w : tap_w + width]
                    * weight_t
                )
    stacked = jnp.stack(taps, axis=3)
    return stacked.reshape(frames * height * width, -1)


def shards(clip_video, clip_ids, norm_gain, conv_weight, out_cotangent):
    video = clip_video[0]
    frames, height, width, channels = video.shape
    outputs = conv_weight.shape[1]
    activated = activate(video, norm_gain).astype(jnp.bfloat16)
    both = jnp.concatenate([video, out_cotangent[0]], axis=-1)
    first_behind = lax.ppermute(both, "tm", ring_route("tm", 1))
    previous = activate(first_behind[..., :channels], norm_gain).astype(jnp.bfloat16)
    extended = jnp.concatenate([previous, activated])
    chain_len = lax.axis_size("tm")
    scale = 1.0 / math.sqrt(lax.axis_size(DATA) * chain_len * frames * height * width)
    kernel_rows = conv_weight.shape[0]
    slab_rows = kernel_rows // chain_len
    slab_start = lax.axis_index("tm") * slab_rows
    tap_lo = slab_start // channels
    slab_offset = slab_start - tap_lo * channels
    group_mask = make_mask(clip_ids[0], 0, frames * chain_len).astype(jnp.bfloat16)
    tap_count = max(
        -(-(slab_rows * index % channels + slab_rows) // channels) for index in range(chain_len)
    )
    tap_params = []
    for step in range(tap_count):
        tap = jnp.minimum(tap_lo + step, 26)
        tap_params.append((tap // 9, tap // 3 % 3, tap % 3))
    me = lax.axis_index("tm")
    blocks = [None] * chain_len
    block_acts = [None] * chain_len
    blocks[0], block_acts[0] = both, activated
    blocks[-1], block_acts[-1] = first_behind, previous

    def block_term(rel):
        ext_pad = jnp.pad(
            jnp.concatenate([block_acts[rel - 1], block_acts[rel]]),
            ((0, 0), (1, 1), (1, 1), (0, 0)),
        )
        owner = (me + rel) % chain_len
        block_mask = lax.dynamic_slice_in_dim(group_mask, owner * frames, frames, 0)
        columns = []
        for tap_t, tap_h, tap_w in tap_params:
            window = lax.dynamic_slice(
                ext_pad, (tap_t, tap_h, tap_w, 0), (frames, height, width, channels)
            )
            weight_t = lax.dynamic_index_in_dim(block_mask, tap_t, 1, keepdims=False)
            columns.append((window * weight_t[:, None, None, None]).reshape(-1, channels))
        block_cot = blocks[rel][..., channels:].reshape(-1, outputs)
        return lax.dot_general(
            block_cot,
            jnp.concatenate(columns, axis=1),
            (((0,), (0,)), ((), ())),
            preferred_element_type=jnp.float32,
        )

    def forward_section(extended, conv_weight):
        first_frame = lax.axis_index("tm") * frames
        tap_mask = make_mask(clip_ids[0], first_frame, frames)
        kernel = conv_weight.reshape(3, 3, 3, channels, outputs)
        tap_scale = tap_mask[:, :, None, None, None]
        taps = jnp.stack([extended[tap_t : tap_t + frames] for tap_t in range(3)], axis=1)
        masked_taps = taps * tap_scale.astype(taps.dtype)
        conv_rows = lax.conv_general_dilated(
            masked_taps,
            kernel,
            (1, 1, 1),
            ((0, 0), (1, 1), (1, 1)),
            dimension_numbers=("NDHWC", "DHWIO", "NDHWC"),
            preferred_element_type=jnp.float32,
        ).astype(jnp.bfloat16)
        return conv_rows

    def backward_section(cotangent, conv_weight, video):
        first_frame = lax.axis_index("tm") * frames
        tap_mask = make_mask(clip_ids[0], first_frame, frames)
        kernel = conv_weight.reshape(3, 3, 3, channels, outputs)
        tap_scale = tap_mask[:, :, None, None, None]
        taps_grad = lax.conv_general_dilated(
            cotangent[:, None],
            kernel[::-1, ::-1, ::-1],
            (1, 1, 1),
            ((2, 2), (1, 1), (1, 1)),
            dimension_numbers=("NDHWC", "DHWOI", "NDHWC"),
            preferred_element_type=jnp.float32,
        )
        masked_grad = taps_grad * tap_scale
        extended_grad = sum(
            jnp.pad(masked_grad[:, tap_t], ((tap_t, 2 - tap_t), (0, 0), (0, 0), (0, 0)))
            for tap_t in range(3)
        )
        returned = from_behind(extended_grad[:2], "tm", -1)
        own_grad = extended_grad[2:] + returned
        unused, pull_norm = jax.vjp(lambda field: activate(field, norm_gain), video.astype(jnp.float32))
        video_grad = pull_norm(own_grad)[0].astype(jnp.bfloat16)
        return video_grad

    pending = list(range(chain_len))

    def add_ready(total):
        for rel in list(pending):
            if block_acts[rel] is not None and block_acts[rel - 1] is not None:
                term = block_term(rel)
                total = term if total is None else total + term
                pending.remove(rel)
        return total

    total = None
    conv_inputs = (extended, conv_weight)
    grad_inputs = (out_cotangent[0], conv_weight, video)
    forward_steps = chain_len // 2
    backward_steps = chain_len - 1 - forward_steps
    forward_moving = first_behind
    backward_moving = lax.ppermute(both, "tm", ring_route("tm", -1))
    arrived = [(chain_len - 1, None), (1, backward_moving)]
    for step in range(2, forward_steps + 1):
        total = add_ready(total)
        if step == 3:
            forward_moving, backward_moving, total, conv_inputs = lax.optimization_barrier(
                (forward_moving, backward_moving, total, conv_inputs)
            )
            conv_rows = forward_section(*conv_inputs)
        elif step == 4:
            forward_moving, backward_moving, total, conv_rows, grad_inputs = (
                lax.optimization_barrier(
                    (forward_moving, backward_moving, total, conv_rows, grad_inputs)
                )
            )
        elif step == 5:
            forward_moving, backward_moving, total, grad_inputs = lax.optimization_barrier(
                (forward_moving, backward_moving, total, grad_inputs)
            )
            video_grad = backward_section(*grad_inputs)
        elif step == 6:
            forward_moving, backward_moving, total, video_grad = lax.optimization_barrier(
                (forward_moving, backward_moving, total, video_grad)
            )
        elif total is not None:
            forward_moving, backward_moving, total = lax.optimization_barrier(
                (forward_moving, backward_moving, total)
            )
        for rel, block in arrived:
            if block is not None:
                blocks[rel] = block
                block_acts[rel] = activate(block[..., :channels], norm_gain).astype(jnp.bfloat16)
        forward_moving = lax.ppermute(forward_moving, "tm", ring_route("tm", 1))
        arrived = [(chain_len - step, forward_moving)]
        if step <= backward_steps:
            backward_moving = lax.ppermute(backward_moving, "tm", ring_route("tm", -1))
            arrived.append((step, backward_moving))
    for rel, block in arrived:
        blocks[rel] = block
        block_acts[rel] = activate(block[..., :channels], norm_gain).astype(jnp.bfloat16)
    total = add_ready(total)
    slab_t = lax.dynamic_slice_in_dim(total, slab_offset, slab_rows, 1)
    chips = lax.axis_size("dq")
    cores = lax.axis_size("dc")
    pieces = slab_t.reshape(chips, cores, outputs // (chips * cores), slab_rows)
    core = lax.axis_index("dc")
    kept = lax.dynamic_index_in_dim(pieces, core, 1, keepdims=False)
    sent = lax.dynamic_index_in_dim(pieces, 1 - core, 1, keepdims=False)
    pair_sum = kept + lax.ppermute(sent, "dc", [(0, 1), (1, 0)])
    reduced_t = lax.all_to_all(pair_sum.astype(jnp.bfloat16), "dq", 0, 0, tiled=False).astype(
        jnp.float32
    ).sum(axis=0)
    grad_weight = reduced_t.T * scale
    conv_out = conv_rows.reshape(1, frames, height, width, outputs)
    return (conv_out, video_grad[None], grad_weight)


def solution(mesh):
    devices = mesh.devices.reshape(mesh.shape["tm"], -1, 2)
    split_mesh = Mesh(devices, ("tm", "dq", "dc"))
    in_specs = (
        P(DATA, "tm", None, None, None),
        P(DATA, None),
        P(),
        P(),
        P(DATA, "tm", None, None, None),
    )
    out_specs = (
        P(DATA, "tm", None, None, None),
        P(DATA, "tm", None, None, None),
        P("tm", DATA),
    )
    return jax.shard_map(
        shards, mesh=split_mesh, in_specs=in_specs, out_specs=out_specs, check_vma=False
    )
```

```python
import math

import jax
import jax.numpy as jnp
from jax import lax
from jax.sharding import Mesh, PartitionSpec as P

DATA = ("dq", "dc")


def from_behind(block, axis, distance):
    devices = range(lax.axis_size(axis))
    route = [(i - distance, i) for i in devices if i - distance in devices]
    return lax.ppermute(block, axis, route)


def ring_route(axis, step):
    size = lax.axis_size(axis)
    return [(i, (i + step) % size) for i in range(size)]


def ring_blocks(block, axis, first_behind):
    size = lax.axis_size(axis)
    relative = [None] * size
    relative[0] = block
    relative[size - 1] = first_behind
    moving = first_behind
    for step in range(2, size // 2 + 1):
        moving = lax.ppermute(moving, axis, ring_route(axis, 1))
        relative[size - step] = moving
    moving = block
    for step in range(1, size - size // 2):
        moving = lax.ppermute(moving, axis, ring_route(axis, -1))
        relative[step] = moving
    return relative


def activate(video, norm_gain):
    values = video.astype(jnp.float32)
    mean_square = jnp.mean(values * values, axis=-1, keepdims=True)
    normed = values * lax.rsqrt(mean_square + 1e-06) * norm_gain
    return jax.nn.silu(normed)


def make_mask(clips, first_frame, count):
    padded_ids = jnp.concatenate([jnp.full((2,), -1, jnp.int32), clips])
    window = lax.dynamic_slice_in_dim(padded_ids, first_frame, count + 2)
    offsets = jnp.arange(count)[:, None] + jnp.arange(3)[None, :]
    current = window[jnp.arange(count) + 2][:, None]
    return (window[offsets] == current).astype(jnp.float32)


def extract(extended, tap_mask):
    frames = tap_mask.shape[0]
    height, width = (extended.shape[1], extended.shape[2])
    padded = jnp.pad(extended, ((0, 0), (1, 1), (1, 1), (0, 0)))
    taps = []
    for tap_t in range(3):
        weight_t = tap_mask[:, tap_t][:, None, None, None].astype(extended.dtype)
        for tap_h in range(3):
            for tap_w in range(3):
                taps.append(
                    padded[tap_t : tap_t + frames, tap_h : tap_h + height, tap_w : tap_w + width]
                    * weight_t
                )
    stacked = jnp.stack(taps, axis=3)
    return stacked.reshape(frames * height * width, -1)


def shards(clip_video, clip_ids, norm_gain, conv_weight, out_cotangent):
    video = clip_video[0]
    frames, height, width, channels = video.shape
    outputs = conv_weight.shape[1]
    activated = activate(video, norm_gain).astype(jnp.bfloat16)
    both = jnp.concatenate([video, out_cotangent[0]], axis=-1)
    block_shape = both.shape
    dense = both.reshape(-1, 128)
    dense_behind = lax.ppermute(dense, "tm", ring_route("tm", 1))
    first_behind = dense_behind.reshape(block_shape)
    previous = activate(first_behind[..., :channels], norm_gain).astype(jnp.bfloat16)
    extended = jnp.concatenate([previous, activated])
    chain_len = lax.axis_size("tm")
    scale = 1.0 / math.sqrt(lax.axis_size(DATA) * chain_len * frames * height * width)
    kernel_rows = conv_weight.shape[0]
    slab_rows = kernel_rows // chain_len
    slab_start = lax.axis_index("tm") * slab_rows
    tap_lo = slab_start // channels
    slab_offset = slab_start - tap_lo * channels
    group_mask = make_mask(clip_ids[0], 0, frames * chain_len).astype(jnp.bfloat16)
    tap_count = max(
        -(-(slab_rows * index % channels + slab_rows) // channels) for index in range(chain_len)
    )
    tap_params = []
    for step in range(tap_count):
        tap = jnp.minimum(tap_lo + step, 26)
        tap_params.append((tap // 9, tap // 3 % 3, tap % 3))
    me = lax.axis_index("tm")
    blocks = [None] * chain_len
    block_acts = [None] * chain_len
    blocks[0], block_acts[0] = both, activated
    blocks[-1], block_acts[-1] = first_behind, previous

    def block_term(rel):
        ext_pad = jnp.pad(
            jnp.concatenate([block_acts[rel - 1], block_acts[rel]]),
            ((0, 0), (1, 1), (1, 1), (0, 0)),
        )
        owner = (me + rel) % chain_len
        block_mask = lax.dynamic_slice_in_dim(group_mask, owner * frames, frames, 0)
        columns = []
        for tap_t, tap_h, tap_w in tap_params:
            window = lax.dynamic_slice(
                ext_pad, (tap_t, tap_h, tap_w, 0), (frames, height, width, channels)
            )
            weight_t = lax.dynamic_index_in_dim(block_mask, tap_t, 1, keepdims=False)
            columns.append((window * weight_t[:, None, None, None]).reshape(-1, channels))
        block_cot = blocks[rel][..., channels:].reshape(-1, outputs)
        return lax.dot_general(
            block_cot,
            jnp.concatenate(columns, axis=1),
            (((0,), (0,)), ((), ())),
            preferred_element_type=jnp.float32,
        )

    def forward_section(extended, conv_weight):
        first_frame = lax.axis_index("tm") * frames
        tap_mask = make_mask(clip_ids[0], first_frame, frames)
        kernel = conv_weight.reshape(3, 3, 3, channels, outputs)
        tap_scale = tap_mask[:, :, None, None, None]
        taps = jnp.stack([extended[tap_t : tap_t + frames] for tap_t in range(3)], axis=1)
        masked_taps = taps * tap_scale.astype(taps.dtype)
        conv_rows = lax.conv_general_dilated(
            masked_taps,
            kernel,
            (1, 1, 1),
            ((0, 0), (1, 1), (1, 1)),
            dimension_numbers=("NDHWC", "DHWIO", "NDHWC"),
            preferred_element_type=jnp.float32,
        ).astype(jnp.bfloat16)
        return conv_rows

    def backward_section(cotangent, conv_weight, video):
        first_frame = lax.axis_index("tm") * frames
        tap_mask = make_mask(clip_ids[0], first_frame, frames)
        kernel = conv_weight.reshape(3, 3, 3, channels, outputs)
        tap_scale = tap_mask[:, :, None, None, None]
        taps_grad = lax.conv_general_dilated(
            cotangent[:, None],
            kernel[::-1, ::-1, ::-1],
            (1, 1, 1),
            ((2, 2), (1, 1), (1, 1)),
            dimension_numbers=("NDHWC", "DHWOI", "NDHWC"),
            preferred_element_type=jnp.float32,
        )
        masked_grad = taps_grad * tap_scale
        extended_grad = sum(
            jnp.pad(masked_grad[:, tap_t], ((tap_t, 2 - tap_t), (0, 0), (0, 0), (0, 0)))
            for tap_t in range(3)
        )
        returned = from_behind(extended_grad[:2], "tm", -1)
        own_grad = extended_grad[2:] + returned
        unused, pull_norm = jax.vjp(lambda field: activate(field, norm_gain), video.astype(jnp.float32))
        video_grad = pull_norm(own_grad)[0].astype(jnp.bfloat16)
        return video_grad

    pending = list(range(chain_len))

    def add_ready(total):
        for rel in list(pending):
            if block_acts[rel] is not None and block_acts[rel - 1] is not None:
                term = block_term(rel)
                total = term if total is None else total + term
                pending.remove(rel)
        return total

    total = None
    conv_inputs = (extended, conv_weight)
    grad_inputs = (out_cotangent[0], conv_weight, video)
    forward_steps = chain_len // 2
    backward_steps = chain_len - 1 - forward_steps
    forward_moving = dense_behind
    backward_moving = lax.ppermute(dense, "tm", ring_route("tm", -1))
    arrived = [(chain_len - 1, None), (1, backward_moving)]
    for step in range(2, forward_steps + 1):
        total = add_ready(total)
        if step == 3:
            forward_moving, backward_moving, total, conv_inputs = lax.optimization_barrier(
                (forward_moving, backward_moving, total, conv_inputs)
            )
            conv_rows = forward_section(*conv_inputs)
        elif step == 4:
            forward_moving, backward_moving, total, conv_rows, grad_inputs = (
                lax.optimization_barrier(
                    (forward_moving, backward_moving, total, conv_rows, grad_inputs)
                )
            )
        elif step == 5:
            forward_moving, backward_moving, total, grad_inputs = lax.optimization_barrier(
                (forward_moving, backward_moving, total, grad_inputs)
            )
            video_grad = backward_section(*grad_inputs)
        elif step == 6:
            forward_moving, backward_moving, total, video_grad = lax.optimization_barrier(
                (forward_moving, backward_moving, total, video_grad)
            )
        elif total is not None:
            forward_moving, backward_moving, total = lax.optimization_barrier(
                (forward_moving, backward_moving, total)
            )
        for rel, block in arrived:
            if block is not None:
                blocks[rel] = block = block.reshape(block_shape)
                block_acts[rel] = activate(block[..., :channels], norm_gain).astype(jnp.bfloat16)
        forward_moving = lax.ppermute(forward_moving, "tm", ring_route("tm", 1))
        arrived = [(chain_len - step, forward_moving)]
        if step <= backward_steps:
            backward_moving = lax.ppermute(backward_moving, "tm", ring_route("tm", -1))
            arrived.append((step, backward_moving))
    for rel, block in arrived:
        blocks[rel] = block = block.reshape(block_shape)
        block_acts[rel] = activate(block[..., :channels], norm_gain).astype(jnp.bfloat16)
    total = add_ready(total)
    slab_t = lax.dynamic_slice_in_dim(total, slab_offset, slab_rows, 1)
    chips = lax.axis_size("dq")
    cores = lax.axis_size("dc")
    pieces = slab_t.reshape(chips, cores, outputs // (chips * cores), slab_rows)
    core = lax.axis_index("dc")
    kept = lax.dynamic_index_in_dim(pieces, core, 1, keepdims=False)
    sent = lax.dynamic_index_in_dim(pieces, 1 - core, 1, keepdims=False)
    pair_sum = kept + lax.ppermute(sent, "dc", [(0, 1), (1, 0)])
    reduced_t = lax.all_to_all(pair_sum.astype(jnp.bfloat16), "dq", 0, 0, tiled=False).astype(
        jnp.float32
    ).sum(axis=0)
    grad_weight = reduced_t.T * scale
    conv_out = conv_rows.reshape(1, frames, height, width, outputs)
    return (conv_out, video_grad[None], grad_weight)


def solution(mesh):
    devices = mesh.devices.reshape(mesh.shape["tm"], -1, 2)
    split_mesh = Mesh(devices, ("tm", "dq", "dc"))
    in_specs = (
        P(DATA, "tm", None, None, None),
        P(DATA, None),
        P(),
        P(),
        P(DATA, "tm", None, None, None),
    )
    out_specs = (
        P(DATA, "tm", None, None, None),
        P(DATA, "tm", None, None, None),
        P("tm", DATA),
    )
    return jax.shard_map(
        shards, mesh=split_mesh, in_specs=in_specs, out_specs=out_specs, check_vma=False
    )
```

```python
import math

import jax
import jax.numpy as jnp
from jax import lax
from jax.sharding import Mesh, PartitionSpec as P

DATA = ("dq", "dc")


def from_behind(block, axis, distance):
    devices = range(lax.axis_size(axis))
    route = [(i - distance, i) for i in devices if i - distance in devices]
    return lax.ppermute(block, axis, route)


def ring_route(axis, step):
    size = lax.axis_size(axis)
    return [(i, (i + step) % size) for i in range(size)]


def ring_blocks(block, axis, first_behind):
    size = lax.axis_size(axis)
    relative = [None] * size
    relative[0] = block
    relative[size - 1] = first_behind
    moving = first_behind
    for step in range(2, size // 2 + 1):
        moving = lax.ppermute(moving, axis, ring_route(axis, 1))
        relative[size - step] = moving
    moving = block
    for step in range(1, size - size // 2):
        moving = lax.ppermute(moving, axis, ring_route(axis, -1))
        relative[step] = moving
    return relative


def activate(video, norm_gain):
    values = video.astype(jnp.float32)
    mean_square = jnp.mean(values * values, axis=-1, keepdims=True)
    normed = values * lax.rsqrt(mean_square + 1e-06) * norm_gain
    return jax.nn.silu(normed)


def make_mask(clips, first_frame, count):
    padded_ids = jnp.concatenate([jnp.full((2,), -1, jnp.int32), clips])
    window = lax.dynamic_slice_in_dim(padded_ids, first_frame, count + 2)
    offsets = jnp.arange(count)[:, None] + jnp.arange(3)[None, :]
    current = window[jnp.arange(count) + 2][:, None]
    return (window[offsets] == current).astype(jnp.float32)


def extract(extended, tap_mask):
    frames = tap_mask.shape[0]
    height, width = (extended.shape[1], extended.shape[2])
    padded = jnp.pad(extended, ((0, 0), (1, 1), (1, 1), (0, 0)))
    taps = []
    for tap_t in range(3):
        weight_t = tap_mask[:, tap_t][:, None, None, None].astype(extended.dtype)
        for tap_h in range(3):
            for tap_w in range(3):
                taps.append(
                    padded[tap_t : tap_t + frames, tap_h : tap_h + height, tap_w : tap_w + width]
                    * weight_t
                )
    stacked = jnp.stack(taps, axis=3)
    return stacked.reshape(frames * height * width, -1)


def shards(clip_video, clip_ids, norm_gain, conv_weight, out_cotangent):
    video = clip_video[0]
    frames, height, width, channels = video.shape
    outputs = conv_weight.shape[1]
    activated = activate(video, norm_gain).astype(jnp.bfloat16)
    both = jnp.concatenate([video, out_cotangent[0]], axis=-1)
    first_behind = lax.ppermute(both, "tm", ring_route("tm", 1))
    previous = activate(first_behind[..., :channels], norm_gain).astype(jnp.bfloat16)
    extended = jnp.concatenate([previous, activated])
    chain_len = lax.axis_size("tm")
    scale = 1.0 / math.sqrt(lax.axis_size(DATA) * chain_len * frames * height * width)
    kernel_rows = conv_weight.shape[0]
    slab_rows = kernel_rows // chain_len
    slab_start = lax.axis_index("tm") * slab_rows
    tap_lo = slab_start // channels
    slab_offset = slab_start - tap_lo * channels
    group_mask = make_mask(clip_ids[0], 0, frames * chain_len).astype(jnp.bfloat16)
    tap_count = max(
        -(-(slab_rows * index % channels + slab_rows) // channels) for index in range(chain_len)
    )
    tap_params = []
    for step in range(tap_count):
        tap = jnp.minimum(tap_lo + step, 26)
        tap_params.append((tap // 9, tap // 3 % 3, tap % 3))
    me = lax.axis_index("tm")
    blocks = [None] * chain_len
    block_acts = [None] * chain_len
    blocks[0], block_acts[0] = both, activated
    blocks[-1], block_acts[-1] = first_behind, previous

    def block_term(rel):
        ext_pad = jnp.pad(
            jnp.concatenate([block_acts[rel - 1], block_acts[rel]]),
            ((0, 0), (1, 1), (1, 1), (0, 0)),
        )
        owner = (me + rel) % chain_len
        block_mask = lax.dynamic_slice_in_dim(group_mask, owner * frames, frames, 0)
        columns = []
        for tap_t, tap_h, tap_w in tap_params:
            window = lax.dynamic_slice(
                ext_pad, (tap_t, tap_h, tap_w, 0), (frames, height, width, channels)
            )
            weight_t = lax.dynamic_index_in_dim(block_mask, tap_t, 1, keepdims=False)
            columns.append((window * weight_t[:, None, None, None]).reshape(-1, channels))
        block_cot = blocks[rel][..., channels:].reshape(-1, outputs)
        return lax.dot_general(
            block_cot,
            jnp.concatenate(columns, axis=1),
            (((0,), (0,)), ((), ())),
            preferred_element_type=jnp.float32,
        )

    def forward_section(extended, conv_weight):
        first_frame = lax.axis_index("tm") * frames
        tap_mask = make_mask(clip_ids[0], first_frame, frames)
        kernel = conv_weight.reshape(3, 3, 3, channels, outputs)
        tap_scale = tap_mask[:, :, None, None, None]
        taps = jnp.stack([extended[tap_t : tap_t + frames] for tap_t in range(3)], axis=1)
        masked_taps = taps * tap_scale.astype(taps.dtype)
        conv_rows = lax.conv_general_dilated(
            masked_taps,
            kernel,
            (1, 1, 1),
            ((0, 0), (1, 1), (1, 1)),
            dimension_numbers=("NDHWC", "DHWIO", "NDHWC"),
            preferred_element_type=jnp.float32,
        ).astype(jnp.bfloat16)
        return conv_rows

    def backward_section(cotangent, conv_weight, video):
        first_frame = lax.axis_index("tm") * frames
        tap_mask = make_mask(clip_ids[0], first_frame, frames)
        kernel = conv_weight.reshape(3, 3, 3, channels, outputs)
        tap_scale = tap_mask[:, :, None, None, None]
        taps_grad = lax.conv_general_dilated(
            cotangent[:, None],
            kernel[::-1, ::-1, ::-1],
            (1, 1, 1),
            ((2, 2), (1, 1), (1, 1)),
            dimension_numbers=("NDHWC", "DHWOI", "NDHWC"),
            preferred_element_type=jnp.float32,
        )
        masked_grad = taps_grad * tap_scale
        extended_grad = sum(
            jnp.pad(masked_grad[:, tap_t], ((tap_t, 2 - tap_t), (0, 0), (0, 0), (0, 0)))
            for tap_t in range(3)
        )
        returned = from_behind(extended_grad[:2], "tm", -1)
        own_grad = extended_grad[2:] + returned
        unused, pull_norm = jax.vjp(lambda field: activate(field, norm_gain), video.astype(jnp.float32))
        video_grad = pull_norm(own_grad)[0].astype(jnp.bfloat16)
        return video_grad

    pending = list(range(chain_len))

    def add_ready(total):
        for rel in list(pending):
            if block_acts[rel] is not None and block_acts[rel - 1] is not None:
                term = block_term(rel)
                total = term if total is None else total + term
                pending.remove(rel)
        return total

    total = None
    conv_inputs = (extended, conv_weight)
    grad_inputs = (out_cotangent[0], conv_weight, video)
    forward_steps = chain_len // 2
    backward_steps = chain_len - 1 - forward_steps
    forward_moving = first_behind
    backward_moving = lax.ppermute(both, "tm", ring_route("tm", -1))
    arrived = [(chain_len - 1, None), (1, backward_moving)]
    for step in range(2, forward_steps + 1):
        total = add_ready(total)
        if step == 3:
            forward_moving, backward_moving, total, conv_inputs = lax.optimization_barrier(
                (forward_moving, backward_moving, total, conv_inputs)
            )
            conv_rows = forward_section(*conv_inputs)
        elif step == 4:
            forward_moving, backward_moving, total, conv_rows, grad_inputs = (
                lax.optimization_barrier(
                    (forward_moving, backward_moving, total, conv_rows, grad_inputs)
                )
            )
        elif step == 5:
            forward_moving, backward_moving, total, grad_inputs = lax.optimization_barrier(
                (forward_moving, backward_moving, total, grad_inputs)
            )
            video_grad = backward_section(*grad_inputs)
        elif step == 6:
            forward_moving, backward_moving, total, video_grad = lax.optimization_barrier(
                (forward_moving, backward_moving, total, video_grad)
            )
        elif total is not None and step > 2:
            forward_moving, backward_moving, total = lax.optimization_barrier(
                (forward_moving, backward_moving, total)
            )
        for rel, block in arrived:
            if block is not None:
                blocks[rel] = block
                block_acts[rel] = activate(block[..., :channels], norm_gain).astype(jnp.bfloat16)
        forward_moving = lax.ppermute(forward_moving, "tm", ring_route("tm", 1))
        arrived = [(chain_len - step, forward_moving)]
        if step <= backward_steps:
            backward_moving = lax.ppermute(backward_moving, "tm", ring_route("tm", -1))
            arrived.append((step, backward_moving))
    for rel, block in arrived:
        blocks[rel] = block
        block_acts[rel] = activate(block[..., :channels], norm_gain).astype(jnp.bfloat16)
    total = add_ready(total)
    slab_t = lax.dynamic_slice_in_dim(total, slab_offset, slab_rows, 1)
    chips = lax.axis_size("dq")
    cores = lax.axis_size("dc")
    pieces = slab_t.reshape(chips, cores, outputs // (chips * cores), slab_rows)
    core = lax.axis_index("dc")
    kept = lax.dynamic_index_in_dim(pieces, core, 1, keepdims=False)
    sent = lax.dynamic_index_in_dim(pieces, 1 - core, 1, keepdims=False)
    pair_sum = kept + lax.ppermute(sent, "dc", [(0, 1), (1, 0)])
    reduced_t = lax.all_to_all(pair_sum.astype(jnp.bfloat16), "dq", 0, 0, tiled=False).astype(
        jnp.float32
    ).sum(axis=0)
    grad_weight = reduced_t.T * scale
    conv_out = conv_rows.reshape(1, frames, height, width, outputs)
    return (conv_out, video_grad[None], grad_weight)


def solution(mesh):
    devices = mesh.devices.reshape(mesh.shape["tm"], -1, 2)
    split_mesh = Mesh(devices, ("tm", "dq", "dc"))
    in_specs = (
        P(DATA, "tm", None, None, None),
        P(DATA, None),
        P(),
        P(),
        P(DATA, "tm", None, None, None),
    )
    out_specs = (
        P(DATA, "tm", None, None, None),
        P(DATA, "tm", None, None, None),
        P("tm", DATA),
    )
    return jax.shard_map(
        shards, mesh=split_mesh, in_specs=in_specs, out_specs=out_specs, check_vma=False
    )
```

```python
import math

import jax
import jax.numpy as jnp
from jax import lax
from jax.sharding import Mesh, PartitionSpec as P

DATA = ("dq", "dc")


def from_behind(block, axis, distance):
    devices = range(lax.axis_size(axis))
    route = [(i - distance, i) for i in devices if i - distance in devices]
    return lax.ppermute(block, axis, route)


def ring_route(axis, step):
    size = lax.axis_size(axis)
    return [(i, (i + step) % size) for i in range(size)]


def ring_blocks(block, axis, first_behind):
    size = lax.axis_size(axis)
    relative = [None] * size
    relative[0] = block
    relative[size - 1] = first_behind
    moving = first_behind
    for step in range(2, size // 2 + 1):
        moving = lax.ppermute(moving, axis, ring_route(axis, 1))
        relative[size - step] = moving
    moving = block
    for step in range(1, size - size // 2):
        moving = lax.ppermute(moving, axis, ring_route(axis, -1))
        relative[step] = moving
    return relative


def activate(video, norm_gain):
    values = video.astype(jnp.float32)
    mean_square = jnp.mean(values * values, axis=-1, keepdims=True)
    normed = values * lax.rsqrt(mean_square + 1e-06) * norm_gain
    return jax.nn.silu(normed)


def make_mask(clips, first_frame, count):
    padded_ids = jnp.concatenate([jnp.full((2,), -1, jnp.int32), clips])
    window = lax.dynamic_slice_in_dim(padded_ids, first_frame, count + 2)
    offsets = jnp.arange(count)[:, None] + jnp.arange(3)[None, :]
    current = window[jnp.arange(count) + 2][:, None]
    return (window[offsets] == current).astype(jnp.float32)


def extract(extended, tap_mask):
    frames = tap_mask.shape[0]
    height, width = (extended.shape[1], extended.shape[2])
    padded = jnp.pad(extended, ((0, 0), (1, 1), (1, 1), (0, 0)))
    taps = []
    for tap_t in range(3):
        weight_t = tap_mask[:, tap_t][:, None, None, None].astype(extended.dtype)
        for tap_h in range(3):
            for tap_w in range(3):
                taps.append(
                    padded[tap_t : tap_t + frames, tap_h : tap_h + height, tap_w : tap_w + width]
                    * weight_t
                )
    stacked = jnp.stack(taps, axis=3)
    return stacked.reshape(frames * height * width, -1)


def shards(clip_video, clip_ids, norm_gain, conv_weight, out_cotangent):
    video = clip_video[0]
    frames, height, width, channels = video.shape
    outputs = conv_weight.shape[1]
    activated = activate(video, norm_gain).astype(jnp.bfloat16)
    both = jnp.concatenate([video, out_cotangent[0]], axis=-1)
    first_behind = lax.ppermute(both, "tm", ring_route("tm", 1))
    previous = activate(first_behind[..., :channels], norm_gain).astype(jnp.bfloat16)
    extended = jnp.concatenate([previous, activated])
    chain_len = lax.axis_size("tm")
    scale = 1.0 / math.sqrt(lax.axis_size(DATA) * chain_len * frames * height * width)
    kernel_rows = conv_weight.shape[0]
    slab_rows = kernel_rows // chain_len
    slab_start = lax.axis_index("tm") * slab_rows
    tap_lo = slab_start // channels
    slab_offset = slab_start - tap_lo * channels
    group_mask = make_mask(clip_ids[0], 0, frames * chain_len).astype(jnp.bfloat16)
    tap_count = max(
        -(-(slab_rows * index % channels + slab_rows) // channels) for index in range(chain_len)
    )
    tap_params = []
    for step in range(tap_count):
        tap = jnp.minimum(tap_lo + step, 26)
        tap_params.append((tap // 9, tap // 3 % 3, tap % 3))
    me = lax.axis_index("tm")
    blocks = [None] * chain_len
    block_acts = [None] * chain_len
    blocks[0], block_acts[0] = both, activated
    blocks[-1], block_acts[-1] = first_behind, previous

    def block_term(rel):
        ext_pad = jnp.pad(
            jnp.concatenate([block_acts[rel - 1], block_acts[rel]]),
            ((0, 0), (1, 1), (1, 1), (0, 0)),
        )
        owner = (me + rel) % chain_len
        block_mask = lax.dynamic_slice_in_dim(group_mask, owner * frames, frames, 0)
        columns = []
        for tap_t, tap_h, tap_w in tap_params:
            window = lax.dynamic_slice(
                ext_pad, (tap_t, tap_h, tap_w, 0), (frames, height, width, channels)
            )
            weight_t = lax.dynamic_index_in_dim(block_mask, tap_t, 1, keepdims=False)
            columns.append((window * weight_t[:, None, None, None]).reshape(-1, channels))
        block_cot = blocks[rel][..., channels:].reshape(-1, outputs)
        return lax.dot_general(
            block_cot,
            jnp.concatenate(columns, axis=1),
            (((0,), (0,)), ((), ())),
            preferred_element_type=jnp.float32,
        )

    def forward_section(extended, conv_weight):
        first_frame = lax.axis_index("tm") * frames
        tap_mask = make_mask(clip_ids[0], first_frame, frames)
        kernel = conv_weight.reshape(3, 3, 3, channels, outputs)
        tap_scale = tap_mask[:, :, None, None, None]
        taps = jnp.stack([extended[tap_t : tap_t + frames] for tap_t in range(3)], axis=1)
        masked_taps = taps * tap_scale.astype(taps.dtype)
        conv_rows = lax.conv_general_dilated(
            masked_taps,
            kernel,
            (1, 1, 1),
            ((0, 0), (1, 1), (1, 1)),
            dimension_numbers=("NDHWC", "DHWIO", "NDHWC"),
            preferred_element_type=jnp.float32,
        ).astype(jnp.bfloat16)
        return conv_rows

    def backward_section(cotangent, conv_weight, video):
        first_frame = lax.axis_index("tm") * frames
        tap_mask = make_mask(clip_ids[0], first_frame, frames)
        kernel = conv_weight.reshape(3, 3, 3, channels, outputs)
        tap_scale = tap_mask[:, :, None, None, None]
        taps_grad = lax.conv_general_dilated(
            cotangent[:, None],
            kernel[::-1, ::-1, ::-1],
            (1, 1, 1),
            ((2, 2), (1, 1), (1, 1)),
            dimension_numbers=("NDHWC", "DHWOI", "NDHWC"),
            preferred_element_type=jnp.float32,
        )
        masked_grad = taps_grad * tap_scale
        extended_grad = sum(
            jnp.pad(masked_grad[:, tap_t], ((tap_t, 2 - tap_t), (0, 0), (0, 0), (0, 0)))
            for tap_t in range(3)
        )
        returned = from_behind(extended_grad[:2], "tm", -1)
        own_grad = extended_grad[2:] + returned
        unused, pull_norm = jax.vjp(lambda field: activate(field, norm_gain), video.astype(jnp.float32))
        video_grad = pull_norm(own_grad)[0].astype(jnp.bfloat16)
        return video_grad

    pending = list(range(chain_len))

    def add_ready(total):
        for rel in list(pending):
            if block_acts[rel] is not None and block_acts[rel - 1] is not None:
                term = block_term(rel)
                total = term if total is None else total + term
                pending.remove(rel)
        return total

    total = None
    conv_inputs = (extended, conv_weight)
    grad_inputs = (out_cotangent[0], conv_weight, video)
    forward_steps = chain_len // 2
    backward_steps = chain_len - 1 - forward_steps
    forward_moving = first_behind
    backward_moving = lax.ppermute(both, "tm", ring_route("tm", -1))
    arrived = [(chain_len - 1, None), (1, backward_moving)]
    for step in range(2, forward_steps + 1):
        total = add_ready(total)
        if step == 3:
            forward_moving, backward_moving, total, conv_inputs = lax.optimization_barrier(
                (forward_moving, backward_moving, total, conv_inputs)
            )
            conv_rows = forward_section(*conv_inputs)
        elif step == 4:
            forward_moving, backward_moving, total, conv_rows, grad_inputs = (
                lax.optimization_barrier(
                    (forward_moving, backward_moving, total, conv_rows, grad_inputs)
                )
            )
        elif step == 5:
            forward_moving, backward_moving, total, grad_inputs = lax.optimization_barrier(
                (forward_moving, backward_moving, total, grad_inputs)
            )
        elif step == 6:
            forward_moving, backward_moving, total, grad_inputs = lax.optimization_barrier(
                (forward_moving, backward_moving, total, grad_inputs)
            )
            video_grad = backward_section(*grad_inputs)
        elif total is not None and step > 2:
            forward_moving, backward_moving, total = lax.optimization_barrier(
                (forward_moving, backward_moving, total)
            )
        for rel, block in arrived:
            if block is not None:
                blocks[rel] = block
                block_acts[rel] = activate(block[..., :channels], norm_gain).astype(jnp.bfloat16)
        forward_moving = lax.ppermute(forward_moving, "tm", ring_route("tm", 1))
        arrived = [(chain_len - step, forward_moving)]
        if step <= backward_steps:
            backward_moving = lax.ppermute(backward_moving, "tm", ring_route("tm", -1))
            arrived.append((step, backward_moving))
    for rel, block in arrived:
        blocks[rel] = block
        block_acts[rel] = activate(block[..., :channels], norm_gain).astype(jnp.bfloat16)
    total = add_ready(total)
    total, video_grad = lax.optimization_barrier((total, video_grad))
    slab_t = lax.dynamic_slice_in_dim(total, slab_offset, slab_rows, 1)
    chips = lax.axis_size("dq")
    cores = lax.axis_size("dc")
    pieces = slab_t.reshape(chips, cores, outputs // (chips * cores), slab_rows)
    core = lax.axis_index("dc")
    kept = lax.dynamic_index_in_dim(pieces, core, 1, keepdims=False)
    sent = lax.dynamic_index_in_dim(pieces, 1 - core, 1, keepdims=False)
    pair_sum = kept + lax.ppermute(sent, "dc", [(0, 1), (1, 0)])
    reduced_t = lax.all_to_all(pair_sum.astype(jnp.bfloat16), "dq", 0, 0, tiled=False).astype(
        jnp.float32
    ).sum(axis=0)
    grad_weight = reduced_t.T * scale
    conv_out = conv_rows.reshape(1, frames, height, width, outputs)
    return (conv_out, video_grad[None], grad_weight)


def solution(mesh):
    devices = mesh.devices.reshape(mesh.shape["tm"], -1, 2)
    split_mesh = Mesh(devices, ("tm", "dq", "dc"))
    in_specs = (
        P(DATA, "tm", None, None, None),
        P(DATA, None),
        P(),
        P(),
        P(DATA, "tm", None, None, None),
    )
    out_specs = (
        P(DATA, "tm", None, None, None),
        P(DATA, "tm", None, None, None),
        P("tm", DATA),
    )
    return jax.shard_map(
        shards, mesh=split_mesh, in_specs=in_specs, out_specs=out_specs, check_vma=False
    )
```

```python
import math

import jax
import jax.numpy as jnp
from jax import lax
from jax.sharding import Mesh, PartitionSpec as P

DATA = ("dq", "dc")


def from_behind(block, axis, distance):
    devices = range(lax.axis_size(axis))
    route = [(i - distance, i) for i in devices if i - distance in devices]
    return lax.ppermute(block, axis, route)


def ring_route(axis, step):
    size = lax.axis_size(axis)
    return [(i, (i + step) % size) for i in range(size)]


def ring_blocks(block, axis, first_behind):
    size = lax.axis_size(axis)
    relative = [None] * size
    relative[0] = block
    relative[size - 1] = first_behind
    moving = first_behind
    for step in range(2, size // 2 + 1):
        moving = lax.ppermute(moving, axis, ring_route(axis, 1))
        relative[size - step] = moving
    moving = block
    for step in range(1, size - size // 2):
        moving = lax.ppermute(moving, axis, ring_route(axis, -1))
        relative[step] = moving
    return relative


def activate(video, norm_gain):
    values = video.astype(jnp.float32)
    mean_square = jnp.mean(values * values, axis=-1, keepdims=True)
    normed = values * lax.rsqrt(mean_square + 1e-06) * norm_gain
    return jax.nn.silu(normed)


def make_mask(clips, first_frame, count):
    padded_ids = jnp.concatenate([jnp.full((2,), -1, jnp.int32), clips])
    window = lax.dynamic_slice_in_dim(padded_ids, first_frame, count + 2)
    offsets = jnp.arange(count)[:, None] + jnp.arange(3)[None, :]
    current = window[jnp.arange(count) + 2][:, None]
    return (window[offsets] == current).astype(jnp.float32)


def extract(extended, tap_mask):
    frames = tap_mask.shape[0]
    height, width = (extended.shape[1], extended.shape[2])
    padded = jnp.pad(extended, ((0, 0), (1, 1), (1, 1), (0, 0)))
    taps = []
    for tap_t in range(3):
        weight_t = tap_mask[:, tap_t][:, None, None, None].astype(extended.dtype)
        for tap_h in range(3):
            for tap_w in range(3):
                taps.append(
                    padded[tap_t : tap_t + frames, tap_h : tap_h + height, tap_w : tap_w + width]
                    * weight_t
                )
    stacked = jnp.stack(taps, axis=3)
    return stacked.reshape(frames * height * width, -1)


def shards(clip_video, clip_ids, norm_gain, conv_weight, out_cotangent):
    video = clip_video[0]
    frames, height, width, channels = video.shape
    outputs = conv_weight.shape[1]
    activated = activate(video, norm_gain).astype(jnp.bfloat16)
    both = jnp.concatenate([video, out_cotangent[0]], axis=-1)
    first_behind = lax.ppermute(both, "tm", ring_route("tm", 1))
    previous = activate(first_behind[..., :channels], norm_gain).astype(jnp.bfloat16)
    extended = jnp.concatenate([previous, activated])
    chain_len = lax.axis_size("tm")
    scale = 1.0 / math.sqrt(lax.axis_size(DATA) * chain_len * frames * height * width)
    kernel_rows = conv_weight.shape[0]
    slab_rows = kernel_rows // chain_len
    slab_start = lax.axis_index("tm") * slab_rows
    tap_lo = slab_start // channels
    slab_offset = slab_start - tap_lo * channels
    group_mask = make_mask(clip_ids[0], 0, frames * chain_len).astype(jnp.bfloat16)
    tap_count = max(
        -(-(slab_rows * index % channels + slab_rows) // channels) for index in range(chain_len)
    )
    tap_params = []
    for step in range(tap_count):
        tap = jnp.minimum(tap_lo + step, 26)
        tap_params.append((tap // 9, tap // 3 % 3, tap % 3))
    me = lax.axis_index("tm")
    blocks = [None] * chain_len
    block_acts = [None] * chain_len
    blocks[0], block_acts[0] = both, activated
    blocks[-1], block_acts[-1] = first_behind, previous

    def block_term(rel):
        ext_pad = jnp.pad(
            jnp.concatenate([block_acts[rel - 1], block_acts[rel]]),
            ((0, 0), (1, 1), (1, 1), (0, 0)),
        )
        owner = (me + rel) % chain_len
        block_mask = lax.dynamic_slice_in_dim(group_mask, owner * frames, frames, 0)
        columns = []
        for tap_t, tap_h, tap_w in tap_params:
            window = lax.dynamic_slice(
                ext_pad, (tap_t, tap_h, tap_w, 0), (frames, height, width, channels)
            )
            weight_t = lax.dynamic_index_in_dim(block_mask, tap_t, 1, keepdims=False)
            columns.append((window * weight_t[:, None, None, None]).reshape(-1, channels))
        block_cot = blocks[rel][..., channels:].reshape(-1, outputs)
        return lax.dot_general(
            block_cot,
            jnp.concatenate(columns, axis=1),
            (((0,), (0,)), ((), ())),
            preferred_element_type=jnp.float32,
        )

    def forward_section(extended, conv_weight):
        first_frame = lax.axis_index("tm") * frames
        tap_mask = make_mask(clip_ids[0], first_frame, frames)
        kernel = conv_weight.reshape(3, 3, 3, channels, outputs)
        tap_scale = tap_mask[:, :, None, None, None]
        taps = jnp.stack([extended[tap_t : tap_t + frames] for tap_t in range(3)], axis=1)
        masked_taps = taps * tap_scale.astype(taps.dtype)
        conv_rows = lax.conv_general_dilated(
            masked_taps,
            kernel,
            (1, 1, 1),
            ((0, 0), (1, 1), (1, 1)),
            dimension_numbers=("NDHWC", "DHWIO", "NDHWC"),
            preferred_element_type=jnp.float32,
        ).astype(jnp.bfloat16)
        return conv_rows

    def backward_section(cotangent, conv_weight, video):
        first_frame = lax.axis_index("tm") * frames
        tap_mask = make_mask(clip_ids[0], first_frame, frames)
        kernel = conv_weight.reshape(3, 3, 3, channels, outputs)
        tap_scale = tap_mask[:, :, None, None, None]
        taps_grad = lax.conv_general_dilated(
            cotangent[:, None],
            kernel[::-1, ::-1, ::-1],
            (1, 1, 1),
            ((2, 2), (1, 1), (1, 1)),
            dimension_numbers=("NDHWC", "DHWOI", "NDHWC"),
            preferred_element_type=jnp.float32,
        )
        masked_grad = taps_grad * tap_scale
        extended_grad = sum(
            jnp.pad(masked_grad[:, tap_t], ((tap_t, 2 - tap_t), (0, 0), (0, 0), (0, 0)))
            for tap_t in range(3)
        )
        returned = from_behind(extended_grad[:2], "tm", -1)
        own_grad = extended_grad[2:] + returned
        unused, pull_norm = jax.vjp(lambda field: activate(field, norm_gain), video.astype(jnp.float32))
        video_grad = pull_norm(own_grad)[0].astype(jnp.bfloat16)
        return video_grad

    pending = list(range(chain_len))

    def add_ready(total):
        for rel in list(pending):
            if block_acts[rel] is not None and block_acts[rel - 1] is not None:
                term = block_term(rel)
                total = term if total is None else total + term
                pending.remove(rel)
        return total

    total = None
    conv_inputs = (extended, conv_weight)
    grad_inputs = (out_cotangent[0], conv_weight, video)
    forward_steps = chain_len // 2
    backward_steps = chain_len - 1 - forward_steps
    forward_moving = first_behind
    backward_moving = lax.ppermute(both, "tm", ring_route("tm", -1))
    arrived = [(chain_len - 1, None), (1, backward_moving)]
    for step in range(2, forward_steps + 1):
        total = add_ready(total)
        if step == 3:
            forward_moving, backward_moving, total, conv_inputs = lax.optimization_barrier(
                (forward_moving, backward_moving, total, conv_inputs)
            )
            conv_rows = forward_section(*conv_inputs)
        elif step == 4:
            forward_moving, backward_moving, total, conv_rows, grad_inputs = (
                lax.optimization_barrier(
                    (forward_moving, backward_moving, total, conv_rows, grad_inputs)
                )
            )
        elif step == 5:
            forward_moving, backward_moving, total, grad_inputs = lax.optimization_barrier(
                (forward_moving, backward_moving, total, grad_inputs)
            )
            video_grad = backward_section(*grad_inputs)
        elif step == 6:
            forward_moving, backward_moving, total, video_grad = lax.optimization_barrier(
                (forward_moving, backward_moving, total, video_grad)
            )
        elif total is not None and step > 2:
            forward_moving, backward_moving, total = lax.optimization_barrier(
                (forward_moving, backward_moving, total)
            )
        for rel, block in arrived:
            if block is not None:
                blocks[rel] = block
                block_acts[rel] = activate(block[..., :channels], norm_gain).astype(jnp.bfloat16)
        forward_moving = lax.ppermute(forward_moving, "tm", ring_route("tm", 1))
        arrived = [(chain_len - step, forward_moving)]
        if step <= backward_steps:
            backward_moving = lax.ppermute(backward_moving, "tm", ring_route("tm", -1))
            arrived.append((step, backward_moving))
    for rel, block in arrived:
        blocks[rel] = block
        block_acts[rel] = activate(block[..., :channels], norm_gain).astype(jnp.bfloat16)
    total = add_ready(total)
    slab_t = lax.dynamic_slice_in_dim(total, slab_offset, slab_rows, 1)
    chips = lax.axis_size("dq")
    cores = lax.axis_size("dc")
    pieces = slab_t.reshape(chips, cores, outputs // (chips * cores), slab_rows)
    core = lax.axis_index("dc")
    kept = lax.dynamic_index_in_dim(pieces, core, 1, keepdims=False)
    sent = lax.dynamic_index_in_dim(pieces, 1 - core, 1, keepdims=False)
    pair_sum = kept + lax.ppermute(sent.astype(jnp.bfloat16), "dc", [(0, 1), (1, 0)]).astype(
        jnp.float32
    )
    reduced_t = lax.all_to_all(pair_sum.astype(jnp.bfloat16), "dq", 0, 0, tiled=False).astype(
        jnp.float32
    ).sum(axis=0)
    grad_weight = reduced_t.T * scale
    conv_out = conv_rows.reshape(1, frames, height, width, outputs)
    return (conv_out, video_grad[None], grad_weight)


def solution(mesh):
    devices = mesh.devices.reshape(mesh.shape["tm"], -1, 2)
    split_mesh = Mesh(devices, ("tm", "dq", "dc"))
    in_specs = (
        P(DATA, "tm", None, None, None),
        P(DATA, None),
        P(),
        P(),
        P(DATA, "tm", None, None, None),
    )
    out_specs = (
        P(DATA, "tm", None, None, None),
        P(DATA, "tm", None, None, None),
        P("tm", DATA),
    )
    return jax.shard_map(
        shards, mesh=split_mesh, in_specs=in_specs, out_specs=out_specs, check_vma=False
    )
```

```python
import math

import jax
import jax.numpy as jnp
from jax import lax
from jax.sharding import Mesh, PartitionSpec as P

DATA = ("dq", "dc")


def from_behind(block, axis, distance):
    devices = range(lax.axis_size(axis))
    route = [(i - distance, i) for i in devices if i - distance in devices]
    return lax.ppermute(block, axis, route)


def ring_route(axis, step):
    size = lax.axis_size(axis)
    return [(i, (i + step) % size) for i in range(size)]


def ring_blocks(block, axis, first_behind):
    size = lax.axis_size(axis)
    relative = [None] * size
    relative[0] = block
    relative[size - 1] = first_behind
    moving = first_behind
    for step in range(2, size // 2 + 1):
        moving = lax.ppermute(moving, axis, ring_route(axis, 1))
        relative[size - step] = moving
    moving = block
    for step in range(1, size - size // 2):
        moving = lax.ppermute(moving, axis, ring_route(axis, -1))
        relative[step] = moving
    return relative


def activate(video, norm_gain):
    values = video.astype(jnp.float32)
    mean_square = jnp.mean(values * values, axis=-1, keepdims=True)
    normed = values * lax.rsqrt(mean_square + 1e-06) * norm_gain
    return jax.nn.silu(normed)


def make_mask(clips, first_frame, count):
    padded_ids = jnp.concatenate([jnp.full((2,), -1, jnp.int32), clips])
    window = lax.dynamic_slice_in_dim(padded_ids, first_frame, count + 2)
    offsets = jnp.arange(count)[:, None] + jnp.arange(3)[None, :]
    current = window[jnp.arange(count) + 2][:, None]
    return (window[offsets] == current).astype(jnp.float32)


def extract(extended, tap_mask):
    frames = tap_mask.shape[0]
    height, width = (extended.shape[1], extended.shape[2])
    padded = jnp.pad(extended, ((0, 0), (1, 1), (1, 1), (0, 0)))
    taps = []
    for tap_t in range(3):
        weight_t = tap_mask[:, tap_t][:, None, None, None].astype(extended.dtype)
        for tap_h in range(3):
            for tap_w in range(3):
                taps.append(
                    padded[tap_t : tap_t + frames, tap_h : tap_h + height, tap_w : tap_w + width]
                    * weight_t
                )
    stacked = jnp.stack(taps, axis=3)
    return stacked.reshape(frames * height * width, -1)


def shards(clip_video, clip_ids, norm_gain, conv_weight, out_cotangent):
    video = clip_video[0]
    frames, height, width, channels = video.shape
    outputs = conv_weight.shape[1]
    activated = activate(video, norm_gain).astype(jnp.bfloat16)
    both = jnp.concatenate([video, out_cotangent[0]], axis=-1)
    first_behind = lax.ppermute(both, "tm", ring_route("tm", 1))
    previous = activate(first_behind[..., :channels], norm_gain).astype(jnp.bfloat16)
    extended = jnp.concatenate([previous, activated])
    chain_len = lax.axis_size("tm")
    scale = 1.0 / math.sqrt(lax.axis_size(DATA) * chain_len * frames * height * width)
    kernel_rows = conv_weight.shape[0]
    slab_rows = kernel_rows // chain_len
    slab_start = lax.axis_index("tm") * slab_rows
    tap_lo = slab_start // channels
    slab_offset = slab_start - tap_lo * channels
    group_mask = make_mask(clip_ids[0], 0, frames * chain_len).astype(jnp.bfloat16)
    tap_count = max(
        -(-(slab_rows * index % channels + slab_rows) // channels) for index in range(chain_len)
    )
    tap_params = []
    for step in range(tap_count):
        tap = jnp.minimum(tap_lo + step, 26)
        tap_params.append((tap // 9, tap // 3 % 3, tap % 3))
    me = lax.axis_index("tm")
    blocks = [None] * chain_len
    block_acts = [None] * chain_len
    blocks[0], block_acts[0] = both, activated
    blocks[-1], block_acts[-1] = first_behind, previous

    def block_term(rel):
        ext_pad = jnp.pad(
            jnp.concatenate([block_acts[rel - 1], block_acts[rel]]),
            ((0, 0), (1, 1), (1, 1), (0, 0)),
        )
        owner = (me + rel) % chain_len
        block_mask = lax.dynamic_slice_in_dim(group_mask, owner * frames, frames, 0)
        columns = []
        for tap_t, tap_h, tap_w in tap_params:
            window = lax.dynamic_slice(
                ext_pad, (tap_t, tap_h, tap_w, 0), (frames, height, width, channels)
            )
            weight_t = lax.dynamic_index_in_dim(block_mask, tap_t, 1, keepdims=False)
            columns.append((window * weight_t[:, None, None, None]).reshape(-1, channels))
        block_cot = blocks[rel][..., channels:].reshape(-1, outputs)
        return lax.dot_general(
            block_cot,
            jnp.concatenate(columns, axis=1),
            (((0,), (0,)), ((), ())),
            preferred_element_type=jnp.float32,
        )

    def forward_section(extended, conv_weight):
        first_frame = lax.axis_index("tm") * frames
        tap_mask = make_mask(clip_ids[0], first_frame, frames)
        kernel = conv_weight.reshape(3, 3, 3, channels, outputs)
        tap_scale = tap_mask[:, :, None, None, None]
        taps = jnp.stack([extended[tap_t : tap_t + frames] for tap_t in range(3)], axis=1)
        masked_taps = taps * tap_scale.astype(taps.dtype)
        conv_rows = lax.conv_general_dilated(
            masked_taps,
            kernel,
            (1, 1, 1),
            ((0, 0), (1, 1), (1, 1)),
            dimension_numbers=("NDHWC", "DHWIO", "NDHWC"),
            preferred_element_type=jnp.float32,
        ).astype(jnp.bfloat16)
        return conv_rows

    def backward_section(cotangent, conv_weight, video):
        first_frame = lax.axis_index("tm") * frames
        tap_mask = make_mask(clip_ids[0], first_frame, frames)
        kernel = conv_weight.reshape(3, 3, 3, channels, outputs)
        tap_scale = tap_mask[:, :, None, None, None]
        taps_grad = lax.conv_general_dilated(
            cotangent[:, None],
            kernel[::-1, ::-1, ::-1],
            (1, 1, 1),
            ((2, 2), (1, 1), (1, 1)),
            dimension_numbers=("NDHWC", "DHWOI", "NDHWC"),
            preferred_element_type=jnp.float32,
        )
        masked_grad = taps_grad * tap_scale
        extended_grad = sum(
            jnp.pad(masked_grad[:, tap_t], ((tap_t, 2 - tap_t), (0, 0), (0, 0), (0, 0)))
            for tap_t in range(3)
        )
        returned = from_behind(extended_grad[:2], "tm", -1)
        own_grad = extended_grad[2:] + returned
        unused, pull_norm = jax.vjp(lambda field: activate(field, norm_gain), video.astype(jnp.float32))
        video_grad = pull_norm(own_grad)[0].astype(jnp.bfloat16)
        return video_grad

    pending = list(range(chain_len))

    def add_ready(total):
        for rel in list(pending):
            if block_acts[rel] is not None and block_acts[rel - 1] is not None:
                term = block_term(rel)
                total = term if total is None else total + term
                pending.remove(rel)
        return total

    total = None
    conv_inputs = (extended, conv_weight)
    grad_inputs = (out_cotangent[0], conv_weight, video)
    forward_steps = chain_len // 2
    backward_steps = chain_len - 1 - forward_steps
    forward_moving = first_behind
    backward_moving = lax.ppermute(both, "tm", ring_route("tm", -1))
    arrived = [(chain_len - 1, None), (1, backward_moving)]
    for step in range(2, forward_steps + 1):
        total = add_ready(total)
        if step == 3:
            forward_moving, backward_moving, total, conv_inputs = lax.optimization_barrier(
                (forward_moving, backward_moving, total, conv_inputs)
            )
            conv_rows = forward_section(*conv_inputs)
        elif step == 4:
            forward_moving, backward_moving, total, conv_rows, grad_inputs = (
                lax.optimization_barrier(
                    (forward_moving, backward_moving, total, conv_rows, grad_inputs)
                )
            )
        elif step == 5:
            forward_moving, backward_moving, total, grad_inputs = lax.optimization_barrier(
                (forward_moving, backward_moving, total, grad_inputs)
            )
            video_grad = backward_section(*grad_inputs)
        elif step == 6:
            forward_moving, backward_moving, total, video_grad = lax.optimization_barrier(
                (forward_moving, backward_moving, total, video_grad)
            )
        elif total is not None and step > 2:
            forward_moving, backward_moving, total = lax.optimization_barrier(
                (forward_moving, backward_moving, total)
            )
        for rel, block in arrived:
            if block is not None:
                blocks[rel] = block
                block_acts[rel] = activate(block[..., :channels], norm_gain).astype(jnp.bfloat16)
        if step > backward_steps and frames > 1:
            half = frames // 2
            front = lax.ppermute(forward_moving[:half], "tm", ring_route("tm", 1))
            back = lax.ppermute(backward_moving[half:], "tm", ring_route("tm", -1))
            arrived = [(chain_len - step, jnp.concatenate([front, back]))]
            continue
        forward_moving = lax.ppermute(forward_moving, "tm", ring_route("tm", 1))
        arrived = [(chain_len - step, forward_moving)]
        if step <= backward_steps:
            backward_moving = lax.ppermute(backward_moving, "tm", ring_route("tm", -1))
            arrived.append((step, backward_moving))
    for rel, block in arrived:
        blocks[rel] = block
        block_acts[rel] = activate(block[..., :channels], norm_gain).astype(jnp.bfloat16)
    total = add_ready(total)
    slab_t = lax.dynamic_slice_in_dim(total, slab_offset, slab_rows, 1)
    chips = lax.axis_size("dq")
    cores = lax.axis_size("dc")
    pieces = slab_t.reshape(chips, cores, outputs // (chips * cores), slab_rows)
    core = lax.axis_index("dc")
    kept = lax.dynamic_index_in_dim(pieces, core, 1, keepdims=False)
    sent = lax.dynamic_index_in_dim(pieces, 1 - core, 1, keepdims=False)
    pair_sum = kept + lax.ppermute(sent, "dc", [(0, 1), (1, 0)])
    reduced_t = lax.all_to_all(pair_sum.astype(jnp.bfloat16), "dq", 0, 0, tiled=False).astype(
        jnp.float32
    ).sum(axis=0)
    grad_weight = reduced_t.T * scale
    conv_out = conv_rows.reshape(1, frames, height, width, outputs)
    return (conv_out, video_grad[None], grad_weight)


def solution(mesh):
    devices = mesh.devices.reshape(mesh.shape["tm"], -1, 2)
    split_mesh = Mesh(devices, ("tm", "dq", "dc"))
    in_specs = (
        P(DATA, "tm", None, None, None),
        P(DATA, None),
        P(),
        P(),
        P(DATA, "tm", None, None, None),
    )
    out_specs = (
        P(DATA, "tm", None, None, None),
        P(DATA, "tm", None, None, None),
        P("tm", DATA),
    )
    return jax.shard_map(
        shards, mesh=split_mesh, in_specs=in_specs, out_specs=out_specs, check_vma=False
    )
```
